256 devices in a mesh: seq: 32 (over y, x, z_hi), tp: 8 (over z_lo, core).
Axes of the slice: x: 4, y: 4, z: 8 (z_hi: 2, z_lo: 4; z = z_hi * 4 + z_lo), core: 2. Of those that a mesh axis runs over, the one named last changes fastest.
Arguments:
- conv_in: bfloat16 [8192, 16384], P('seq', 'tp'), may hold values from -6 to 6
- gate_in: bfloat16 [8192, 16384], P('seq', 'tp'), may hold values from -6 to 6
- q_proj: bfloat16 [8192, 8192], P('seq', 'tp'), may hold values from -6 to 6
- k_proj: bfloat16 [8192, 1024], P('seq', 'tp'), may hold values from -6 to 6
- v_proj: bfloat16 [8192, 1024], P('seq', 'tp'), may hold values from -6 to 6
- conv_weight: float32 [4, 16384], P(None, 'tp'), may hold values from -3 to 3
- conv_bias: float32 [16384], P('tp'), may hold values from -0.5 to 0.5
- proj_dt_weight: bfloat16 [16384, 512], P('tp'), may hold values from -0.046875 to 0.046875
- proj_bc_weight: bfloat16 [32, 16384], P(None, 'tp'), may hold values from -0.046875 to 0.046875
- dt_gain: float32 [512], replicated, may hold values from 0.1 to 1.9
- dt_weight: bfloat16 [512, 16384], P(None, 'tp'), may hold values from -0.25 to 0.25
- dt_bias: float32 [16384], P('tp'), may hold values from -5 to -2
- decay_rate: float32 [16, 16384], P(None, 'tp'), may hold values from 1e-05 to 2
- skip_weight: float32 [16384], P('tp'), may hold values from 0.5 to 1.5
Outputs:
- mamba_out: bfloat16 [8192, 16384], P('seq', 'tp')
- attn_out: bfloat16 [8192, 8192], P('seq', 'tp')
The draws below stay inside these ranges and needn't reach their ends.
All inputs are finite; a program needn't handle non-finite values.
Results may differ from the reference program's by a relative error of at most 0.0051.
Values may be sent and summed in bfloat16 or wider, within the bound.
No kernel may reach another device: no remote copies, remote signals or barrier semaphores. Data moves between devices by JAX's collectives and lax.ppermute only.
A program may use at most 128 MiB of HBM per device.

```python
import math
import jax
import jax.numpy as jnp
from jax import lax

E = 16384
NSTATE = 16
KCONV = 4
RANK = 512
H = 64
KVH = 8
HD = 128
TOK_DEV = 256
WINDOW = 2048
TOKENS = 8192


def draw_k_proj(key, part):
    shape_keys = (TOKENS, KVH, HD)
    values = jnp.clip(jax.random.normal(jax.random.fold_in(key, 2), shape_keys, jnp.float32), -6.0, 6.0)
    return values.reshape(TOKENS, KVH * HD).astype(jnp.bfloat16)


def draw_q_proj(key, part):
    shape_queries = (TOKENS, KVH, H // KVH, HD)
    values = jnp.clip(jax.random.normal(jax.random.fold_in(key, 1), shape_queries, jnp.float32), -6.0, 6.0)
    return values.reshape(TOKENS, H * HD).astype(jnp.bfloat16)


def level_of(own_key, extent, cuts, least, largest):
    loudness = 1.0
    for axis_at, parts in cuts:
        heights = jax.random.uniform(jax.random.fold_in(jax.random.fold_in(own_key, 6), axis_at), (parts,), jnp.float32, least / len(cuts), largest / len(cuts))
        loudness = loudness * jnp.repeat(jnp.exp(heights), extent[axis_at] // parts).reshape((-1,) + (1,) * (len(extent) - 1 - axis_at))
    return loudness


def gaussian(key, dims, deviation, limit, pieces=(), kind=jnp.bfloat16):
    gain = level_of(key, dims, pieces, -0.22, 0.18) if pieces else 1.0
    drawn = jax.random.normal(key, dims, jnp.float32) * deviation * gain
    return jnp.minimum(jnp.maximum(drawn, -limit), limit).astype(kind)


def setup_inputs(seed: int = 0) -> dict:
    seeds = jax.random.split(jax.random.key(seed), 15)
    return {
        "conv_in": gaussian(seeds[0], (TOKENS, E), 1.0, 6.0, ((0, 32), (1, 8))),
        "gate_in": gaussian(seeds[1], (TOKENS, E), 1.0, 6.0, ((0, 32), (1, 8))),
        "q_proj": draw_q_proj(jax.random.fold_in(seeds[14], 71), 0),
        "k_proj": draw_k_proj(jax.random.fold_in(seeds[14], 71), 0),
        "v_proj": gaussian(seeds[4], (TOKENS, KVH * HD), 1.0, 6.0, ((0, 32), (1, 8))),
        "conv_weight": gaussian(seeds[5], (KCONV, E), KCONV ** -0.5, 3.0, ((1, 8),), jnp.float32),
        "conv_bias": jnp.clip(jax.random.uniform(seeds[6], (E,), jnp.float32, -0.5, 0.5) * level_of(seeds[6], (E,), ((0, 8),), -0.4, 0.0), -0.5, 0.5),
        "proj_dt_weight": gaussian(seeds[7], (E, RANK), E ** -0.5, 0.046875, ((0, 8),)),
        "proj_bc_weight": gaussian(seeds[8], (2 * NSTATE, E), E ** -0.5, 0.046875, ((1, 8),)),
        "dt_gain": jnp.clip(1.0 + 0.18 * jax.random.normal(seeds[9], (RANK,), jnp.float32), 0.1, 1.9),
        "dt_weight": gaussian(seeds[10], (RANK, E), RANK ** -0.5, 0.25, ((1, 8),)),
        "dt_bias": jnp.clip(-5.0 + 3.0 * jax.random.uniform(seeds[11], (E,), jnp.float32) ** level_of(seeds[11], (E,), ((0, 8),), -0.2, 0.2), -5.0, -2.0),
        "decay_rate": jnp.clip(jnp.exp(math.log(2.0) - 12.206073 * jax.random.uniform(seeds[12], (NSTATE, E), jnp.float32) ** level_of(seeds[12], (NSTATE, E), ((1, 8),), -0.2, 0.2)), 9.999999747378752e-06, 2.0),
        "skip_weight": jnp.clip(0.5 + 1.0 * jax.random.uniform(seeds[13], (E,), jnp.float32) ** level_of(seeds[13], (E,), ((0, 8),), -0.2, 0.2), 0.5, 1.5),
    }


epsilon = 1e-06

def causal_conv(padded, conv_weight, conv_bias, length):
    summed = conv_bias[None, :] + jnp.zeros((length, padded.shape[1]), jnp.float32)
    for offset in range(KCONV):
        summed = summed + conv_weight[offset][None, :] * padded[offset:offset + length]
    return jax.nn.silu(summed).astype(jnp.bfloat16)

def rank_norm(rank_low, dt_gain):
    mean_square = lax.optimization_barrier(jnp.mean(rank_low * rank_low, axis=-1, keepdims=True))
    return (rank_low * lax.rsqrt(mean_square + epsilon) * dt_gain[None, :]).astype(jnp.bfloat16)

def mamba_part(conv_in, gate_in, conv_weight, conv_bias, proj_dt_weight, proj_bc_weight, dt_gain, dt_weight, dt_bias, decay_rate, skip_weight):
    tokens_all, channels = conv_in.shape
    block_width = min(2048, channels)
    block_count = channels // block_width

    def conv_block(index_block):
        first_col = (index_block * block_width).astype(jnp.int32)
        inputs_block = lax.dynamic_slice_in_dim(conv_in, first_col, block_width, 1).astype(jnp.float32)
        padded = jnp.concatenate([jnp.zeros((KCONV - 1, block_width), jnp.float32), inputs_block], axis=0)
        taps = lax.dynamic_slice_in_dim(conv_weight, first_col, block_width, 1)
        biases = lax.dynamic_slice_in_dim(conv_bias, first_col, block_width, 0)
        return causal_conv(padded, taps, biases, tokens_all)
    activated = lax.map(conv_block, jnp.arange(block_count, dtype=jnp.int32))

    def add_rank(index_block, carry_pair):
        rank_sum, state_sum = carry_pair
        index_now = jnp.asarray(index_block).astype(jnp.int32)
        first_col = (index_now * block_width).astype(jnp.int32)
        block_values = activated[index_now]
        rank_sum = rank_sum + jnp.dot(block_values, lax.dynamic_slice_in_dim(proj_dt_weight, first_col, block_width, 0), preferred_element_type=jnp.float32)
        state_sum = state_sum + lax.dot_general(lax.dynamic_slice_in_dim(proj_bc_weight, first_col, block_width, 1), block_values, (((1,), (1,)), ((), ())), preferred_element_type=jnp.float32)
        return (rank_sum, state_sum)
    rank_low, state_in = lax.fori_loop(0, block_count, add_rank, (jnp.zeros((tokens_all, RANK), jnp.float32), jnp.zeros((2 * NSTATE, tokens_all), jnp.float32)))
    rank_normed = rank_norm(rank_low, dt_gain)
    input_rows = state_in[:NSTATE]
    output_rows = state_in[NSTATE:]

    def scan_block(index_block):
        first_col = (index_block * block_width).astype(jnp.int32)
        block_values = activated[index_block].astype(jnp.float32)
        step_size = jax.nn.softplus(jnp.dot(rank_normed, lax.dynamic_slice_in_dim(dt_weight, first_col, block_width, 1), preferred_element_type=jnp.float32) + lax.dynamic_slice_in_dim(dt_bias, first_col, block_width, 0)[None, :])
        drive_term = step_size * block_values
        rate_block = lax.dynamic_slice_in_dim(decay_rate, first_col, block_width, 1)

        def advance(hidden_state, inputs_now):
            step_now, drive_now, input_now, output_now = inputs_now
            hidden_state = jnp.exp(-rate_block * step_now[None, :]) * hidden_state + input_now[:, None] * drive_now[None, :]
            return (hidden_state, lax.optimization_barrier(jnp.sum(output_now[:, None] * hidden_state, axis=0)))
        final_state, outputs = lax.scan(advance, jnp.zeros((NSTATE, block_width), jnp.float32), (step_size, drive_term, input_rows.T, output_rows.T))
        gate_block = lax.dynamic_slice_in_dim(gate_in, first_col, block_width, 1).astype(jnp.float32)
        skip_block = lax.dynamic_slice_in_dim(skip_weight, first_col, block_width, 0)
        return ((outputs + skip_block[None, :] * block_values) * jax.nn.silu(gate_block)).astype(jnp.bfloat16)
    mixed = lax.map(scan_block, jnp.arange(block_count, dtype=jnp.int32))
    return mixed.transpose(1, 0, 2).reshape(tokens_all, channels)

def attention_part(q_proj, k_proj, v_proj):
    tokens_all = q_proj.shape[0]
    grouping = H // KVH
    queries = q_proj.reshape(tokens_all, KVH, grouping, HD)
    keys_pad = jnp.concatenate([jnp.zeros((WINDOW, KVH * HD), k_proj.dtype), k_proj], axis=0).reshape(WINDOW + tokens_all, KVH, HD)
    values_pad = jnp.concatenate([jnp.zeros((WINDOW, KVH * HD), v_proj.dtype), v_proj], axis=0).reshape(WINDOW + tokens_all, KVH, HD)
    block_count = tokens_all // TOK_DEV

    def one_block(index_block):
        first_row = (index_block * TOK_DEV).astype(jnp.int32)
        query_block = lax.dynamic_slice_in_dim(queries, first_row, TOK_DEV, 0).astype(jnp.float32)
        key_block = lax.dynamic_slice_in_dim(keys_pad, first_row, WINDOW + TOK_DEV, 0).astype(jnp.float32)
        value_block = lax.dynamic_slice_in_dim(values_pad, first_row, WINDOW + TOK_DEV, 0).astype(jnp.float32)
        scores = jnp.einsum('tkgd,skd->kgts', query_block, key_block) * (1.0 / math.sqrt(HD))
        row_ids = jnp.arange(TOK_DEV, dtype=jnp.int32)[:, None]
        col_ids = jnp.arange(WINDOW + TOK_DEV, dtype=jnp.int32)[None, :]
        distance = WINDOW + row_ids - col_ids
        in_window = (distance >= 0) & (distance < WINDOW) & (col_ids + first_row >= WINDOW)
        row_peak = lax.optimization_barrier(jnp.max(jnp.where(in_window, scores, -jnp.inf), axis=-1, keepdims=True))
        weights = jnp.exp(jnp.where(in_window, scores - row_peak, -jnp.inf)).astype(jnp.bfloat16)
        summed = lax.optimization_barrier(jnp.sum(weights.astype(jnp.float32), axis=-1))
        weighted = jnp.einsum('kgts,skd->tkgd', weights.astype(jnp.float32), value_block)
        result = weighted / summed.transpose(2, 0, 1)[..., None]
        return result.astype(jnp.bfloat16).reshape(TOK_DEV, H * HD)
    return lax.map(one_block, jnp.arange(block_count, dtype=jnp.int32)).reshape(tokens_all, H * HD)

def reference(conv_in, gate_in, q_proj, k_proj, v_proj, conv_weight, conv_bias, proj_dt_weight, proj_bc_weight, dt_gain, dt_weight, dt_bias, decay_rate, skip_weight):
    mamba_out = mamba_part(conv_in, gate_in, conv_weight, conv_bias, proj_dt_weight, proj_bc_weight, dt_gain, dt_weight, dt_bias, decay_rate, skip_weight)
    attn_out = attention_part(q_proj, k_proj, v_proj)
    return (mamba_out, attn_out)
```

```python
import functools
import math

import jax
import jax.numpy as jnp
from jax import lax
from jax.experimental import pallas as pl
from jax.experimental.pallas import tpu as pltpu
from jax.sharding import PartitionSpec as P

KCONV = 4
HD = 128
WINDOW = 2048
SUBLANES = 8
LANE_BLOCK = 128
epsilon = 1e-06


def shifted(value, axis, steps):
    count = lax.axis_size(axis)
    first, last = (max(0, -steps), min(count, count - steps))
    return lax.ppermute(value, axis, [(source, source + steps) for source in range(first, last)])


def causal_conv(padded, conv_weight, conv_bias, length):
    summed = conv_bias[None, :] + jnp.zeros((length, padded.shape[1]), jnp.float32)
    for offset in range(KCONV):
        summed = summed + conv_weight[offset][None, :] * padded[offset : offset + length]
    return jax.nn.silu(summed).astype(jnp.bfloat16)


def rank_norm(rank_low, dt_gain):
    mean_square = jnp.mean(rank_low * rank_low, axis=-1, keepdims=True)
    return (rank_low * lax.rsqrt(mean_square + epsilon) * dt_gain[None, :]).astype(jnp.bfloat16)


def scan_kernel(with_out, bc_ref, dt_ref, dr_ref, rate_ref, h0_ref, out_ref):
    states = rate_ref.shape[0]
    tokens = dt_ref.shape[0]
    neg_rate = [-rate_ref[n] for n in range(states)]

    def body(t, hs):
        dt = dt_ref[t]
        dr = dr_ref[t]
        new = []
        acc = None
        for n in range(states):
            h = jnp.exp(neg_rate[n] * dt) * hs[n] + bc_ref[n, t] * dr
            new.append(h)
            if with_out:
                term = bc_ref[states + n, t] * h
                acc = term if acc is None else acc + term
        if with_out:
            out_ref[t] = acc
        return tuple(new)

    hs = lax.fori_loop(0, tokens, body, tuple(h0_ref[n] for n in range(states)), unroll=2)
    if not with_out:
        for n in range(states):
            out_ref[n] = hs[n]


def run_scan(bc, dt3, dr3, rate3, h0, with_out):
    tokens, sub, lanes = dt3.shape
    states = rate3.shape[0]
    blocks = lanes // LANE_BLOCK
    row_spec = pl.BlockSpec((tokens, sub, LANE_BLOCK), lambda j: (0, 0, j))
    state_spec = pl.BlockSpec((states, sub, LANE_BLOCK), lambda j: (0, 0, j))
    out_shape = (tokens, sub, lanes) if with_out else (states, sub, lanes)
    elems = tokens * states * sub * lanes
    return pl.pallas_call(
        functools.partial(scan_kernel, with_out),
        grid=(blocks,),
        in_specs=[
            pl.BlockSpec(memory_space=pltpu.SMEM),
            row_spec,
            row_spec,
            state_spec,
            state_spec,
        ],
        out_specs=row_spec if with_out else state_spec,
        out_shape=jax.ShapeDtypeStruct(out_shape, jnp.float32),
        cost_estimate=pl.CostEstimate(
            flops=(6 if with_out else 4) * elems,
            transcendentals=elems,
            bytes_accessed=4 * (3 * tokens * sub * lanes + 2 * states * sub * lanes),
        ),
    )(bc, dt3, dr3, rate3, h0)


def entering_state(step_sum, final_state, rate3):
    packed = jnp.concatenate([step_sum[None], final_state], axis=0)
    gathered = lax.all_gather(packed, "seq")
    peers = gathered.shape[0]
    me = lax.axis_index("seq")
    sums = gathered[:, 0]
    states = gathered[:, 1:]
    earlier = jnp.arange(peers) < me
    masked = jnp.where(earlier[:, None, None], sums, 0.0)
    suffix = jnp.cumsum(masked[::-1], axis=0)[::-1]
    between = jnp.concatenate([suffix[1:], jnp.zeros_like(suffix[:1])], axis=0)
    weight = jnp.where(
        earlier[:, None, None, None], jnp.exp(-rate3[None] * between[:, None]), 0.0
    )
    return jnp.sum(weight * states, axis=0)


def per_device(
    conv_in,
    gate_in,
    q_proj,
    k_proj,
    v_proj,
    conv_weight,
    conv_bias,
    proj_dt_weight,
    proj_bc_weight,
    dt_gain,
    dt_weight,
    dt_bias,
    decay_rate,
    skip_weight,
):
    tokens_here, channels = conv_in.shape
    key_span = WINDOW // tokens_here
    conv_tail = conv_in[tokens_here - (KCONV - 1) :]
    neighbour = shifted((k_proj, v_proj, conv_tail), "seq", 1)
    key_blocks = [k_proj, neighbour[0]]
    value_blocks = [v_proj, neighbour[1]]
    for distance in range(2, key_span + 1):
        distant = shifted((k_proj, v_proj), "seq", distance)
        key_blocks.append(distant[0])
        value_blocks.append(distant[1])
    padded = jnp.concatenate([neighbour[2], conv_in], axis=0).astype(jnp.float32)
    activated = causal_conv(padded, conv_weight, conv_bias, tokens_here)
    state_parts = lax.dot_general(
        proj_bc_weight, activated, (((1,), (1,)), ((), ())), preferred_element_type=jnp.float32
    )
    rank_part = jnp.dot(activated, proj_dt_weight, preferred_element_type=jnp.float32)
    rank_low, state_in = lax.psum((rank_part, state_parts), "tp")
    rank_normed = rank_norm(rank_low, dt_gain)
    step_size = jax.nn.softplus(
        jnp.dot(rank_normed, dt_weight, preferred_element_type=jnp.float32) + dt_bias[None, :]
    )
    drive_term = step_size * activated.astype(jnp.float32)
    state_count = decay_rate.shape[0]
    lanes = channels // SUBLANES
    dt3 = step_size.reshape(tokens_here, SUBLANES, lanes)
    dr3 = drive_term.reshape(tokens_here, SUBLANES, lanes)
    rate3 = decay_rate.reshape(state_count, SUBLANES, lanes)
    zero_state = jnp.zeros((state_count, SUBLANES, lanes), jnp.float32)
    local_final = run_scan(state_in, dt3, dr3, rate3, zero_state, False)
    step_sum = jnp.sum(dt3, axis=0)
    entering = entering_state(step_sum, local_final, rate3)
    mamba_sum = run_scan(state_in, dt3, dr3, rate3, entering, True).reshape(tokens_here, channels)
    mamba_out = (
        (mamba_sum + skip_weight[None, :] * activated.astype(jnp.float32))
        * jax.nn.silu(gate_in.astype(jnp.float32))
    ).astype(jnp.bfloat16)
    heads_here = q_proj.shape[1] // HD
    kv_here = k_proj.shape[1] // HD
    grouping = heads_here // kv_here
    keys_all = jnp.concatenate(key_blocks[::-1], axis=0).reshape(-1, kv_here, HD)
    values_all = jnp.concatenate(value_blocks[::-1], axis=0).reshape(-1, kv_here, HD)
    queries = q_proj.reshape(tokens_here, kv_here, grouping, HD)
    scores = jnp.einsum("tkgd,skd->kgts", queries, keys_all, preferred_element_type=jnp.float32) * (
        1.0 / math.sqrt(HD)
    )
    index_seq = lax.axis_index("seq")
    row_ids = jnp.arange(tokens_here, dtype=jnp.int32)[:, None]
    col_ids = jnp.arange((key_span + 1) * tokens_here, dtype=jnp.int32)[None, :]
    distance_all = WINDOW + row_ids - col_ids
    in_window = (
        (distance_all >= 0)
        & (distance_all < WINDOW)
        & (col_ids + index_seq * tokens_here >= WINDOW)
    )
    row_peak = jnp.max(jnp.where(in_window, scores, -jnp.inf), axis=-1, keepdims=True)
    weights = jnp.exp(jnp.where(in_window, scores - row_peak, -jnp.inf)).astype(jnp.bfloat16)
    summed = jnp.sum(weights.astype(jnp.float32), axis=-1)
    weighted = jnp.einsum("kgts,skd->tkgd", weights, values_all, preferred_element_type=jnp.float32)
    attn_out = (
        (weighted / summed.transpose(2, 0, 1)[..., None])
        .astype(jnp.bfloat16)
        .reshape(tokens_here, heads_here * HD)
    )
    return (mamba_out, attn_out)


def solution(mesh):
    return jax.shard_map(
        per_device,
        mesh=mesh,
        in_specs=(
            P("seq", "tp"),
            P("seq", "tp"),
            P("seq", "tp"),
            P("seq", "tp"),
            P("seq", "tp"),
            P(None, "tp"),
            P("tp"),
            P("tp", None),
            P(None, "tp"),
            P(),
            P(None, "tp"),
            P("tp"),
            P(None, "tp"),
            P("tp"),
        ),
        out_specs=(P("seq", "tp"), P("seq", "tp")),
        check_vma=False,
    )
```

```python
import functools
import math

import jax
import jax.numpy as jnp
from jax import lax
from jax.experimental import pallas as pl
from jax.experimental.pallas import tpu as pltpu
from jax.sharding import PartitionSpec as P

KCONV = 4
HD = 128
WINDOW = 2048
SUBLANES = 8
LANE_BLOCK = 128
epsilon = 1e-06


def shifted(value, axis, steps):
    count = lax.axis_size(axis)
    first, last = (max(0, -steps), min(count, count - steps))
    return lax.ppermute(value, axis, [(source, source + steps) for source in range(first, last)])


def causal_conv(padded, conv_weight, conv_bias, length):
    summed = conv_bias[None, :] + jnp.zeros((length, padded.shape[1]), jnp.float32)
    for offset in range(KCONV):
        summed = summed + conv_weight[offset][None, :] * padded[offset : offset + length]
    return jax.nn.silu(summed).astype(jnp.bfloat16)


def rank_norm(rank_low, dt_gain):
    mean_square = jnp.mean(rank_low * rank_low, axis=-1, keepdims=True)
    return (rank_low * lax.rsqrt(mean_square + epsilon) * dt_gain[None, :]).astype(jnp.bfloat16)


def scan_kernel(with_out, bc_ref, dt_ref, dr_ref, rate_ref, h0_ref, out_ref):
    states = rate_ref.shape[0]
    tokens = dt_ref.shape[0]
    neg_rate = [-rate_ref[n] for n in range(states)]

    def body(t, hs):
        dt = dt_ref[t]
        dr = dr_ref[t]
        new = []
        acc = None
        for n in range(states):
            h = jnp.exp(neg_rate[n] * dt) * hs[n] + bc_ref[n, t] * dr
            new.append(h)
            if with_out:
                term = bc_ref[states + n, t] * h
                acc = term if acc is None else acc + term
        if with_out:
            out_ref[t] = acc
        return tuple(new)

    hs = lax.fori_loop(0, tokens, body, tuple(h0_ref[n] for n in range(states)), unroll=2)
    if not with_out:
        for n in range(states):
            out_ref[n] = hs[n]


def run_scan(bc, dt3, dr3, rate3, h0, with_out):
    tokens, sub, lanes = dt3.shape
    states = rate3.shape[0]
    blocks = lanes // LANE_BLOCK
    row_spec = pl.BlockSpec((tokens, sub, LANE_BLOCK), lambda j: (0, 0, j))
    state_spec = pl.BlockSpec((states, sub, LANE_BLOCK), lambda j: (0, 0, j))
    out_shape = (tokens, sub, lanes) if with_out else (states, sub, lanes)
    elems = tokens * states * sub * lanes
    return pl.pallas_call(
        functools.partial(scan_kernel, with_out),
        grid=(blocks,),
        in_specs=[
            pl.BlockSpec(memory_space=pltpu.SMEM),
            row_spec,
            row_spec,
            state_spec,
            state_spec,
        ],
        out_specs=row_spec if with_out else state_spec,
        out_shape=jax.ShapeDtypeStruct(out_shape, jnp.float32),
        cost_estimate=pl.CostEstimate(
            flops=(6 if with_out else 4) * elems,
            transcendentals=elems,
            bytes_accessed=4 * (3 * tokens * sub * lanes + 2 * states * sub * lanes),
        ),
    )(bc, dt3, dr3, rate3, h0)


def compose(earlier, later, rate3):
    decay = jnp.exp(-rate3 * later[0][None])
    states = decay * earlier[1:] + later[1:]
    return jnp.concatenate([(earlier[0] + later[0])[None], states], axis=0)


def entering_state(step_sum, final_state, rate3):
    local = jnp.concatenate([step_sum[None], final_state], axis=0)
    peers = lax.axis_size("seq")
    running = shifted(local, "seq", 1)
    distance = 1
    while distance < peers - 1:
        running = compose(shifted(running, "seq", distance), running, rate3)
        distance *= 2
    return running[1:]


def window_blocks(k_proj, v_proj, conv_tail, key_span):
    tokens = k_proj.shape[0]
    own = jnp.concatenate([k_proj, v_proj], axis=1)
    width = own.shape[1]
    tail = conv_tail.reshape(-1, width)
    first = shifted(jnp.concatenate([own, tail], axis=0), "seq", 1)
    tail_in = first[tokens:].reshape(conv_tail.shape)
    held = [first[:tokens], own]
    reach = 2
    while reach * 2 <= key_span:
        held = [shifted(jnp.concatenate(held, axis=0), "seq", reach)] + held
        reach *= 2
    assert reach == key_span
    held = [shifted(own, "seq", key_span)] + held
    window = jnp.concatenate(held, axis=0)
    half = k_proj.shape[1]
    return window[:, :half], window[:, half:], tail_in


def per_device(
    conv_in,
    gate_in,
    q_proj,
    k_proj,
    v_proj,
    conv_weight,
    conv_bias,
    proj_dt_weight,
    proj_bc_weight,
    dt_gain,
    dt_weight,
    dt_bias,
    decay_rate,
    skip_weight,
):
    tokens_here, channels = conv_in.shape
    key_span = WINDOW // tokens_here
    conv_tail = conv_in[tokens_here - (KCONV - 1) :]
    keys_window, values_window, tail_in = window_blocks(k_proj, v_proj, conv_tail, key_span)
    padded = jnp.concatenate([tail_in, conv_in], axis=0).astype(jnp.float32)
    activated = causal_conv(padded, conv_weight, conv_bias, tokens_here)
    state_parts = lax.dot_general(
        proj_bc_weight, activated, (((1,), (1,)), ((), ())), preferred_element_type=jnp.float32
    )
    rank_part = jnp.dot(activated, proj_dt_weight, preferred_element_type=jnp.float32)
    rank_width = rank_part.shape[1]
    packed = jnp.concatenate([rank_part, state_parts.reshape(-1, rank_width)], axis=0)
    total = lax.psum(packed, "tp")
    rank_low = total[:tokens_here]
    state_in = total[tokens_here:].reshape(state_parts.shape)
    rank_normed = rank_norm(rank_low, dt_gain)
    step_size = jax.nn.softplus(
        jnp.dot(rank_normed, dt_weight, preferred_element_type=jnp.float32) + dt_bias[None, :]
    )
    drive_term = step_size * activated.astype(jnp.float32)
    state_count = decay_rate.shape[0]
    lanes = channels // SUBLANES
    dt3 = step_size.reshape(tokens_here, SUBLANES, lanes)
    dr3 = drive_term.reshape(tokens_here, SUBLANES, lanes)
    rate3 = decay_rate.reshape(state_count, SUBLANES, lanes)
    zero_state = jnp.zeros((state_count, SUBLANES, lanes), jnp.float32)
    local_final = run_scan(state_in, dt3, dr3, rate3, zero_state, False)
    step_sum = jnp.sum(dt3, axis=0)
    entering = entering_state(step_sum, local_final, rate3)
    mamba_sum = run_scan(state_in, dt3, dr3, rate3, entering, True).reshape(tokens_here, channels)
    mamba_out = (
        (mamba_sum + skip_weight[None, :] * activated.astype(jnp.float32))
        * jax.nn.silu(gate_in.astype(jnp.float32))
    ).astype(jnp.bfloat16)
    heads_here = q_proj.shape[1] // HD
    kv_here = k_proj.shape[1] // HD
    grouping = heads_here // kv_here
    keys_all = keys_window.reshape(-1, kv_here, HD)
    values_all = values_window.reshape(-1, kv_here, HD)
    queries = q_proj.reshape(tokens_here, kv_here, grouping, HD)
    scores = jnp.einsum("tkgd,skd->kgts", queries, keys_all, preferred_element_type=jnp.float32) * (
        1.0 / math.sqrt(HD)
    )
    index_seq = lax.axis_index("seq")
    row_ids = jnp.arange(tokens_here, dtype=jnp.int32)[:, None]
    col_ids = jnp.arange((key_span + 1) * tokens_here, dtype=jnp.int32)[None, :]
    distance_all = WINDOW + row_ids - col_ids
    in_window = (
        (distance_all >= 0)
        & (distance_all < WINDOW)
        & (col_ids + index_seq * tokens_here >= WINDOW)
    )
    row_peak = jnp.max(jnp.where(in_window, scores, -jnp.inf), axis=-1, keepdims=True)
    weights = jnp.exp(jnp.where(in_window, scores - row_peak, -jnp.inf)).astype(jnp.bfloat16)
    summed = jnp.sum(weights.astype(jnp.float32), axis=-1)
    weighted = jnp.einsum("kgts,skd->tkgd", weights, values_all, preferred_element_type=jnp.float32)
    attn_out = (
        (weighted / summed.transpose(2, 0, 1)[..., None])
        .astype(jnp.bfloat16)
        .reshape(tokens_here, heads_here * HD)
    )
    return (mamba_out, attn_out)


def solution(mesh):
    return jax.shard_map(
        per_device,
        mesh=mesh,
        in_specs=(
            P("seq", "tp"),
            P("seq", "tp"),
            P("seq", "tp"),
            P("seq", "tp"),
            P("seq", "tp"),
            P(None, "tp"),
            P("tp"),
            P("tp", None),
            P(None, "tp"),
            P(),
            P(None, "tp"),
            P("tp"),
            P(None, "tp"),
            P("tp"),
        ),
        out_specs=(P("seq", "tp"), P("seq", "tp")),
        check_vma=False,
    )
```

```python
import functools
import math

import jax
import jax.numpy as jnp
from jax import lax
from jax.experimental import pallas as pl
from jax.experimental.pallas import tpu as pltpu
from jax.sharding import PartitionSpec as P

KCONV = 4
HD = 128
WINDOW = 2048
SUBLANES = 8
LANE_BLOCK = 128
epsilon = 1e-06


def shifted(value, axis, steps):
    count = lax.axis_size(axis)
    first, last = (max(0, -steps), min(count, count - steps))
    return lax.ppermute(value, axis, [(source, source + steps) for source in range(first, last)])


def causal_conv(padded, conv_weight, conv_bias, length):
    summed = conv_bias[None, :] + jnp.zeros((length, padded.shape[1]), jnp.float32)
    for offset in range(KCONV):
        summed = summed + conv_weight[offset][None, :] * padded[offset : offset + length]
    return jax.nn.silu(summed).astype(jnp.bfloat16)


def rank_norm(rank_low, dt_gain):
    mean_square = jnp.mean(rank_low * rank_low, axis=-1, keepdims=True)
    return (rank_low * lax.rsqrt(mean_square + epsilon) * dt_gain[None, :]).astype(jnp.bfloat16)


def scan_kernel(with_out, bc_ref, dt_ref, dr_ref, rate_ref, h0_ref, out_ref):
    states = rate_ref.shape[0]
    tokens = dt_ref.shape[0]
    neg_rate = [-rate_ref[n] for n in range(states)]

    def body(t, hs):
        dt = dt_ref[t]
        dr = dr_ref[t]
        new = []
        acc = None
        for n in range(states):
            h = jnp.exp(neg_rate[n] * dt) * hs[n] + bc_ref[n, t] * dr
            new.append(h)
            if with_out:
                term = bc_ref[states + n, t] * h
                acc = term if acc is None else acc + term
        if with_out:
            out_ref[t] = acc
        return tuple(new)

    hs = lax.fori_loop(0, tokens, body, tuple(h0_ref[n] for n in range(states)), unroll=2)
    if not with_out:
        for n in range(states):
            out_ref[n] = hs[n]


def run_scan(bc, dt3, dr3, rate3, h0, with_out):
    tokens, sub, lanes = dt3.shape
    states = rate3.shape[0]
    blocks = lanes // LANE_BLOCK
    row_spec = pl.BlockSpec((tokens, sub, LANE_BLOCK), lambda j: (0, 0, j))
    state_spec = pl.BlockSpec((states, sub, LANE_BLOCK), lambda j: (0, 0, j))
    out_shape = (tokens, sub, lanes) if with_out else (states, sub, lanes)
    elems = tokens * states * sub * lanes
    return pl.pallas_call(
        functools.partial(scan_kernel, with_out),
        grid=(blocks,),
        in_specs=[
            pl.BlockSpec(memory_space=pltpu.SMEM),
            row_spec,
            row_spec,
            state_spec,
            state_spec,
        ],
        out_specs=row_spec if with_out else state_spec,
        out_shape=jax.ShapeDtypeStruct(out_shape, jnp.float32),
        cost_estimate=pl.CostEstimate(
            flops=(6 if with_out else 4) * elems,
            transcendentals=elems,
            bytes_accessed=4 * (3 * tokens * sub * lanes + 2 * states * sub * lanes),
        ),
    )(bc, dt3, dr3, rate3, h0)


def butterfly_sum(value, axis):
    count = lax.axis_size(axis)
    stride = 1
    while stride < count:
        pairs = [(source, source ^ stride) for source in range(count)]
        value = value + lax.ppermute(value, axis, pairs)
        stride *= 2
    return value


def compose(earlier, later, rate3):
    decay = jnp.exp(-rate3 * later[0][None])
    states = decay * earlier[1:] + later[1:]
    return jnp.concatenate([(earlier[0] + later[0])[None], states], axis=0)


def entering_state(step_sum, final_state, rate3):
    local = jnp.concatenate([step_sum[None], final_state], axis=0)
    peers = lax.axis_size("seq")
    running = shifted(local, "seq", 1)
    distance = 1
    while distance < peers - 1:
        running = compose(shifted(running, "seq", distance), running, rate3)
        distance *= 2
    return running[1:]


def window_blocks(k_proj, v_proj, conv_tail, key_span):
    tokens = k_proj.shape[0]
    own = jnp.concatenate([k_proj, v_proj], axis=1)
    width = own.shape[1]
    tail = conv_tail.reshape(-1, width)
    first = shifted(jnp.concatenate([own, tail], axis=0), "seq", 1)
    tail_in = first[tokens:].reshape(conv_tail.shape)
    held = [first[:tokens], own]
    reach = 2
    while reach * 2 <= key_span:
        held = [shifted(jnp.concatenate(held, axis=0), "seq", reach)] + held
        reach *= 2
    assert reach == key_span
    held = [shifted(own, "seq", key_span)] + held
    window = jnp.concatenate(held, axis=0)
    half = k_proj.shape[1]
    return window[:, :half], window[:, half:], tail_in


def per_device(
    conv_in,
    gate_in,
    q_proj,
    k_proj,
    v_proj,
    conv_weight,
    conv_bias,
    proj_dt_weight,
    proj_bc_weight,
    dt_gain,
    dt_weight,
    dt_bias,
    decay_rate,
    skip_weight,
):
    tokens_here, channels = conv_in.shape
    key_span = WINDOW // tokens_here
    conv_tail = conv_in[tokens_here - (KCONV - 1) :]
    keys_window, values_window, tail_in = window_blocks(k_proj, v_proj, conv_tail, key_span)
    padded = jnp.concatenate([tail_in, conv_in], axis=0).astype(jnp.float32)
    activated = causal_conv(padded, conv_weight, conv_bias, tokens_here)
    state_parts = lax.dot_general(
        proj_bc_weight, activated, (((1,), (1,)), ((), ())), preferred_element_type=jnp.float32
    )
    rank_part = jnp.dot(activated, proj_dt_weight, preferred_element_type=jnp.float32)
    rank_width = rank_part.shape[1]
    packed = jnp.concatenate([rank_part, state_parts.reshape(-1, rank_width)], axis=0)
    total = butterfly_sum(packed, "tp")
    rank_low = total[:tokens_here]
    state_in = total[tokens_here:].reshape(state_parts.shape)
    rank_normed = rank_norm(rank_low, dt_gain)
    step_size = jax.nn.softplus(
        jnp.dot(rank_normed, dt_weight, preferred_element_type=jnp.float32) + dt_bias[None, :]
    )
    drive_term = step_size * activated.astype(jnp.float32)
    state_count = decay_rate.shape[0]
    lanes = channels // SUBLANES
    dt3 = step_size.reshape(tokens_here, SUBLANES, lanes)
    dr3 = drive_term.reshape(tokens_here, SUBLANES, lanes)
    rate3 = decay_rate.reshape(state_count, SUBLANES, lanes)
    zero_state = jnp.zeros((state_count, SUBLANES, lanes), jnp.float32)
    local_final = run_scan(state_in, dt3, dr3, rate3, zero_state, False)
    step_sum = jnp.sum(dt3, axis=0)
    entering = entering_state(step_sum, local_final, rate3)
    mamba_sum = run_scan(state_in, dt3, dr3, rate3, entering, True).reshape(tokens_here, channels)
    mamba_out = (
        (mamba_sum + skip_weight[None, :] * activated.astype(jnp.float32))
        * jax.nn.silu(gate_in.astype(jnp.float32))
    ).astype(jnp.bfloat16)
    heads_here = q_proj.shape[1] // HD
    kv_here = k_proj.shape[1] // HD
    grouping = heads_here // kv_here
    keys_all = keys_window.reshape(-1, kv_here, HD)
    values_all = values_window.reshape(-1, kv_here, HD)
    queries = q_proj.reshape(tokens_here, kv_here, grouping, HD)
    scores = jnp.einsum("tkgd,skd->kgts", queries, keys_all, preferred_element_type=jnp.float32) * (
        1.0 / math.sqrt(HD)
    )
    index_seq = lax.axis_index("seq")
    row_ids = jnp.arange(tokens_here, dtype=jnp.int32)[:, None]
    col_ids = jnp.arange((key_span + 1) * tokens_here, dtype=jnp.int32)[None, :]
    distance_all = WINDOW + row_ids - col_ids
    in_window = (
        (distance_all >= 0)
        & (distance_all < WINDOW)
        & (col_ids + index_seq * tokens_here >= WINDOW)
    )
    row_peak = jnp.max(jnp.where(in_window, scores, -jnp.inf), axis=-1, keepdims=True)
    weights = jnp.exp(jnp.where(in_window, scores - row_peak, -jnp.inf)).astype(jnp.bfloat16)
    summed = jnp.sum(weights.astype(jnp.float32), axis=-1)
    weighted = jnp.einsum("kgts,skd->tkgd", weights, values_all, preferred_element_type=jnp.float32)
    attn_out = (
        (weighted / summed.transpose(2, 0, 1)[..., None])
        .astype(jnp.bfloat16)
        .reshape(tokens_here, heads_here * HD)
    )
    return (mamba_out, attn_out)


def solution(mesh):
    return jax.shard_map(
        per_device,
        mesh=mesh,
        in_specs=(
            P("seq", "tp"),
            P("seq", "tp"),
            P("seq", "tp"),
            P("seq", "tp"),
            P("seq", "tp"),
            P(None, "tp"),
            P("tp"),
            P("tp", None),
            P(None, "tp"),
            P(),
            P(None, "tp"),
            P("tp"),
            P(None, "tp"),
            P("tp"),
        ),
        out_specs=(P("seq", "tp"), P("seq", "tp")),
        check_vma=False,
    )
```

```python
import functools
import math

import jax
import jax.numpy as jnp
from jax import lax
from jax.experimental import pallas as pl
from jax.experimental.pallas import tpu as pltpu
from jax.sharding import PartitionSpec as P

KCONV = 4
HD = 128
WINDOW = 2048
SUBLANES = 8
LANE_BLOCK = 128
epsilon = 1e-06


def shifted(value, axis, steps):
    count = lax.axis_size(axis)
    first, last = (max(0, -steps), min(count, count - steps))
    return lax.ppermute(value, axis, [(source, source + steps) for source in range(first, last)])


def causal_conv(padded, conv_weight, conv_bias, length):
    summed = conv_bias[None, :] + jnp.zeros((length, padded.shape[1]), jnp.float32)
    for offset in range(KCONV):
        summed = summed + conv_weight[offset][None, :] * padded[offset : offset + length]
    return jax.nn.silu(summed).astype(jnp.bfloat16)


def rank_norm(rank_low, dt_gain):
    mean_square = jnp.mean(rank_low * rank_low, axis=-1, keepdims=True)
    return (rank_low * lax.rsqrt(mean_square + epsilon) * dt_gain[None, :]).astype(jnp.bfloat16)


def scan_kernel(with_out, bc_ref, dt_ref, dr_ref, rate_ref, h0_ref, out_ref):
    states = rate_ref.shape[0]
    tokens = dt_ref.shape[0]
    neg_rate = [-rate_ref[n] for n in range(states)]

    def body(t, hs):
        dt = dt_ref[t]
        dr = dr_ref[t]
        new = []
        acc = None
        for n in range(states):
            h = jnp.exp(neg_rate[n] * dt) * hs[n] + bc_ref[n, t] * dr
            new.append(h)
            if with_out:
                term = bc_ref[states + n, t] * h
                acc = term if acc is None else acc + term
        if with_out:
            out_ref[t] = acc
        return tuple(new)

    hs = lax.fori_loop(0, tokens, body, tuple(h0_ref[n] for n in range(states)), unroll=2)
    if not with_out:
        for n in range(states):
            out_ref[n] = hs[n]


def run_scan(bc, dt3, dr3, rate3, h0, with_out):
    tokens, sub, lanes = dt3.shape
    states = rate3.shape[0]
    blocks = lanes // LANE_BLOCK
    row_spec = pl.BlockSpec((tokens, sub, LANE_BLOCK), lambda j: (0, 0, j))
    state_spec = pl.BlockSpec((states, sub, LANE_BLOCK), lambda j: (0, 0, j))
    out_shape = (tokens, sub, lanes) if with_out else (states, sub, lanes)
    elems = tokens * states * sub * lanes
    return pl.pallas_call(
        functools.partial(scan_kernel, with_out),
        grid=(blocks,),
        in_specs=[
            pl.BlockSpec(memory_space=pltpu.SMEM),
            row_spec,
            row_spec,
            state_spec,
            state_spec,
        ],
        out_specs=row_spec if with_out else state_spec,
        out_shape=jax.ShapeDtypeStruct(out_shape, jnp.float32),
        cost_estimate=pl.CostEstimate(
            flops=(6 if with_out else 4) * elems,
            transcendentals=elems,
            bytes_accessed=4 * (3 * tokens * sub * lanes + 2 * states * sub * lanes),
        ),
    )(bc, dt3, dr3, rate3, h0)


def attention_kernel(base_ref, q_ref, k_ref, v_ref, o_ref):
    scores = lax.dot_general(
        q_ref[...], k_ref[...], (((1,), (1,)), ((), ())), preferred_element_type=jnp.float32
    ) * (1.0 / math.sqrt(HD))
    rows = lax.broadcasted_iota(jnp.int32, scores.shape, 0)
    cols = lax.broadcasted_iota(jnp.int32, scores.shape, 1)
    distance = WINDOW + rows - cols
    in_window = (distance >= 0) & (distance < WINDOW) & (cols + base_ref[0] >= WINDOW)
    row_peak = jnp.max(jnp.where(in_window, scores, -jnp.inf), axis=1, keepdims=True)
    weights = jnp.exp(jnp.where(in_window, scores - row_peak, -jnp.inf)).astype(jnp.bfloat16)
    summed = jnp.sum(weights.astype(jnp.float32), axis=1, keepdims=True)
    weighted = jnp.dot(weights, v_ref[...], preferred_element_type=jnp.float32)
    o_ref[...] = (weighted / summed).astype(o_ref.dtype)


def run_attention(q_proj, window, base):
    tokens, width = q_proj.shape
    keys = window.shape[0]
    heads = width // HD
    group = heads // (window.shape[1] // (2 * HD))
    return pl.pallas_call(
        attention_kernel,
        grid=(heads,),
        in_specs=[
            pl.BlockSpec(memory_space=pltpu.SMEM),
            pl.BlockSpec((tokens, HD), lambda h: (0, h)),
            pl.BlockSpec((keys, HD), lambda h: (0, h // group)),
            pl.BlockSpec((keys, HD), lambda h: (0, window.shape[1] // (2 * HD) + h // group)),
        ],
        out_specs=pl.BlockSpec((tokens, HD), lambda h: (0, h)),
        out_shape=jax.ShapeDtypeStruct((tokens, width), q_proj.dtype),
        cost_estimate=pl.CostEstimate(
            flops=4 * tokens * keys * HD * heads,
            transcendentals=tokens * keys * heads,
            bytes_accessed=2 * (2 * tokens * width + 2 * keys * window.shape[1]),
        ),
    )(base, q_proj, window, window)


def butterfly_sum(value, axis):
    count = lax.axis_size(axis)
    stride = 1
    while stride < count:
        pairs = [(source, source ^ stride) for source in range(count)]
        value = value + lax.ppermute(value, axis, pairs)
        stride *= 2
    return value


def compose(earlier, later, rate3):
    decay = jnp.exp(-rate3 * later[0][None])
    states = decay * earlier[1:] + later[1:]
    return jnp.concatenate([(earlier[0] + later[0])[None], states], axis=0)


def entering_state(step_sum, final_state, rate3):
    local = jnp.concatenate([step_sum[None], final_state], axis=0)
    peers = lax.axis_size("seq")
    running = shifted(local, "seq", 1)
    distance = 1
    while distance < peers - 1:
        running = compose(shifted(running, "seq", distance), running, rate3)
        distance *= 2
    return running[1:]


def window_blocks(k_proj, v_proj, conv_tail, key_span):
    tokens = k_proj.shape[0]
    own = jnp.concatenate([k_proj, v_proj], axis=1)
    width = own.shape[1]
    tail = conv_tail.reshape(-1, width)
    first = shifted(jnp.concatenate([own, tail], axis=0), "seq", 1)
    tail_in = first[tokens:].reshape(conv_tail.shape)
    held = [first[:tokens], own]
    reach = 2
    while reach * 2 <= key_span:
        held = [shifted(jnp.concatenate(held, axis=0), "seq", reach)] + held
        reach *= 2
    assert reach == key_span
    held = [shifted(own, "seq", key_span)] + held
    return jnp.concatenate(held, axis=0), tail_in


def per_device(
    conv_in,
    gate_in,
    q_proj,
    k_proj,
    v_proj,
    conv_weight,
    conv_bias,
    proj_dt_weight,
    proj_bc_weight,
    dt_gain,
    dt_weight,
    dt_bias,
    decay_rate,
    skip_weight,
):
    tokens_here, channels = conv_in.shape
    key_span = WINDOW // tokens_here
    conv_tail = conv_in[tokens_here - (KCONV - 1) :]
    window, tail_in = window_blocks(k_proj, v_proj, conv_tail, key_span)
    padded = jnp.concatenate([tail_in, conv_in], axis=0).astype(jnp.float32)
    activated = causal_conv(padded, conv_weight, conv_bias, tokens_here)
    state_parts = lax.dot_general(
        proj_bc_weight, activated, (((1,), (1,)), ((), ())), preferred_element_type=jnp.float32
    )
    rank_part = jnp.dot(activated, proj_dt_weight, preferred_element_type=jnp.float32)
    rank_width = rank_part.shape[1]
    packed = jnp.concatenate([rank_part, state_parts.reshape(-1, rank_width)], axis=0)
    total = butterfly_sum(packed, "tp")
    rank_low = total[:tokens_here]
    state_in = total[tokens_here:].reshape(state_parts.shape)
    rank_normed = rank_norm(rank_low, dt_gain)
    step_size = jax.nn.softplus(
        jnp.dot(rank_normed, dt_weight, preferred_element_type=jnp.float32) + dt_bias[None, :]
    )
    drive_term = step_size * activated.astype(jnp.float32)
    state_count = decay_rate.shape[0]
    lanes = channels // SUBLANES
    dt3 = step_size.reshape(tokens_here, SUBLANES, lanes)
    dr3 = drive_term.reshape(tokens_here, SUBLANES, lanes)
    rate3 = decay_rate.reshape(state_count, SUBLANES, lanes)
    zero_state = jnp.zeros((state_count, SUBLANES, lanes), jnp.float32)
    local_final = run_scan(state_in, dt3, dr3, rate3, zero_state, False)
    step_sum = jnp.sum(dt3, axis=0)
    entering = entering_state(step_sum, local_final, rate3)
    mamba_sum = run_scan(state_in, dt3, dr3, rate3, entering, True).reshape(tokens_here, channels)
    mamba_out = (
        (mamba_sum + skip_weight[None, :] * activated.astype(jnp.float32))
        * jax.nn.silu(gate_in.astype(jnp.float32))
    ).astype(jnp.bfloat16)
    base = (lax.axis_index("seq") * tokens_here).astype(jnp.int32).reshape(1)
    attn_out = run_attention(q_proj, window, base)
    return (mamba_out, attn_out)


def solution(mesh):
    return jax.shard_map(
        per_device,
        mesh=mesh,
        in_specs=(
            P("seq", "tp"),
            P("seq", "tp"),
            P("seq", "tp"),
            P("seq", "tp"),
            P("seq", "tp"),
            P(None, "tp"),
            P("tp"),
            P("tp", None),
            P(None, "tp"),
            P(),
            P(None, "tp"),
            P("tp"),
            P(None, "tp"),
            P("tp"),
        ),
        out_specs=(P("seq", "tp"), P("seq", "tp")),
        check_vma=False,
    )
```

```python
import functools
import math

import jax
import jax.numpy as jnp
from jax import lax
from jax.experimental import pallas as pl
from jax.experimental.pallas import tpu as pltpu
from jax.sharding import PartitionSpec as P

KCONV = 4
HD = 128
WINDOW = 2048
SUBLANES = 8
LANE_BLOCK = 128
epsilon = 1e-06


def shifted(value, axis, steps):
    count = lax.axis_size(axis)
    first, last = (max(0, -steps), min(count, count - steps))
    return lax.ppermute(value, axis, [(source, source + steps) for source in range(first, last)])


def causal_conv(padded, conv_weight, conv_bias, length):
    summed = conv_bias[None, :] + jnp.zeros((length, padded.shape[1]), jnp.float32)
    for offset in range(KCONV):
        summed = summed + conv_weight[offset][None, :] * padded[offset : offset + length]
    return jax.nn.silu(summed).astype(jnp.bfloat16)


def rank_norm(rank_low, dt_gain):
    mean_square = jnp.mean(rank_low * rank_low, axis=-1, keepdims=True)
    return (rank_low * lax.rsqrt(mean_square + epsilon) * dt_gain[None, :]).astype(jnp.bfloat16)


def scan_kernel(with_out, bc_ref, dt_ref, dr_ref, rate_ref, h0_ref, out_ref):
    states = rate_ref.shape[0]
    tokens = dt_ref.shape[0]
    neg_rate = [-rate_ref[n] for n in range(states)]

    def body(t, hs):
        dt = dt_ref[t]
        dr = dr_ref[t]
        new = []
        acc = None
        for n in range(states):
            h = jnp.exp(neg_rate[n] * dt) * hs[n] + bc_ref[n, t] * dr
            new.append(h)
            if with_out:
                term = bc_ref[states + n, t] * h
                acc = term if acc is None else acc + term
        if with_out:
            out_ref[t] = acc
        return tuple(new)

    hs = lax.fori_loop(0, tokens, body, tuple(h0_ref[n] for n in range(states)), unroll=2)
    if not with_out:
        for n in range(states):
            out_ref[n] = hs[n]


def run_scan(bc, dt3, dr3, rate3, h0, with_out):
    tokens, sub, lanes = dt3.shape
    states = rate3.shape[0]
    blocks = lanes // LANE_BLOCK
    row_spec = pl.BlockSpec((tokens, sub, LANE_BLOCK), lambda j: (0, 0, j))
    state_spec = pl.BlockSpec((states, sub, LANE_BLOCK), lambda j: (0, 0, j))
    out_shape = (tokens, sub, lanes) if with_out else (states, sub, lanes)
    elems = tokens * states * sub * lanes
    return pl.pallas_call(
        functools.partial(scan_kernel, with_out),
        grid=(blocks,),
        in_specs=[
            pl.BlockSpec(memory_space=pltpu.SMEM),
            row_spec,
            row_spec,
            state_spec,
            state_spec,
        ],
        out_specs=row_spec if with_out else state_spec,
        out_shape=jax.ShapeDtypeStruct(out_shape, jnp.float32),
        cost_estimate=pl.CostEstimate(
            flops=(6 if with_out else 4) * elems,
            transcendentals=elems,
            bytes_accessed=4 * (3 * tokens * sub * lanes + 2 * states * sub * lanes),
        ),
    )(bc, dt3, dr3, rate3, h0)


def attention_kernel(base_ref, q_ref, k_ref, v_ref, o_ref, bias_ref):
    @pl.when(pl.program_id(0) == 0)
    def _():
        rows = lax.broadcasted_iota(jnp.int32, bias_ref.shape, 0)
        cols = lax.broadcasted_iota(jnp.int32, bias_ref.shape, 1)
        distance = WINDOW + rows - cols
        in_window = (distance >= 0) & (distance < WINDOW) & (cols + base_ref[0] >= WINDOW)
        bias_ref[...] = jnp.where(in_window, 0.0, -jnp.inf)

    scores = lax.dot_general(
        q_ref[...], k_ref[...], (((1,), (1,)), ((), ())), preferred_element_type=jnp.float32
    ) * (1.0 / math.sqrt(HD)) + bias_ref[...]
    row_peak = jnp.max(scores, axis=1, keepdims=True)
    weights = jnp.exp(scores - row_peak).astype(jnp.bfloat16)
    summed = jnp.sum(weights.astype(jnp.float32), axis=1, keepdims=True)
    weighted = jnp.dot(weights, v_ref[...], preferred_element_type=jnp.float32)
    o_ref[...] = (weighted / summed).astype(o_ref.dtype)


def run_attention(q_proj, window, base):
    tokens, width = q_proj.shape
    keys = window.shape[0]
    heads = width // HD
    group = heads // (window.shape[1] // (2 * HD))
    return pl.pallas_call(
        attention_kernel,
        grid=(heads,),
        in_specs=[
            pl.BlockSpec(memory_space=pltpu.SMEM),
            pl.BlockSpec((tokens, HD), lambda h: (0, h)),
            pl.BlockSpec((keys, HD), lambda h: (0, h // group)),
            pl.BlockSpec((keys, HD), lambda h: (0, window.shape[1] // (2 * HD) + h // group)),
        ],
        out_specs=pl.BlockSpec((tokens, HD), lambda h: (0, h)),
        out_shape=jax.ShapeDtypeStruct((tokens, width), q_proj.dtype),
        scratch_shapes=[pltpu.VMEM((tokens, keys), jnp.float32)],
        cost_estimate=pl.CostEstimate(
            flops=4 * tokens * keys * HD * heads,
            transcendentals=tokens * keys * heads,
            bytes_accessed=2 * (2 * tokens * width + 2 * keys * window.shape[1]),
        ),
    )(base, q_proj, window, window)


def butterfly_sum(value, axis):
    count = lax.axis_size(axis)
    stride = 1
    while stride < count:
        pairs = [(source, source ^ stride) for source in range(count)]
        value = value + lax.ppermute(value, axis, pairs)
        stride *= 2
    return value


def compose(earlier, later, rate3):
    decay = jnp.exp(-rate3 * later[0][None])
    states = decay * earlier[1:] + later[1:]
    return jnp.concatenate([(earlier[0] + later[0])[None], states], axis=0)


def scan_with_window(step_sum, final_state, rate3, own, key_span):
    rows = (final_state.shape[0] + 1) * final_state.shape[1]
    lanes = final_state.shape[2]
    local = jnp.concatenate([step_sum[None], final_state], axis=0).reshape(rows, lanes)
    own = own.astype(jnp.float32)
    tokens = own.shape[0]
    peers = lax.axis_size("seq")

    def merge(received, running):
        earlier = received[:rows].reshape(-1, *final_state.shape[1:])
        later = running.reshape(-1, *final_state.shape[1:])
        return compose(earlier, later, rate3).reshape(rows, lanes)

    first = shifted(jnp.concatenate([local, own], axis=0), "seq", 1)
    running = first[:rows]
    held = [first[rows:]]
    distance = 1
    while distance < peers - 1:
        payload = [running]
        if len(held) < key_span:
            payload = payload + held[-distance:]
        received = shifted(jnp.concatenate(payload, axis=0), "seq", distance)
        if len(held) < key_span:
            count = len(payload) - 1
            held = [received[rows + i * tokens : rows + (i + 1) * tokens] for i in range(count)] + held
        running = merge(received, running)
        distance *= 2
    assert len(held) == key_span
    window = jnp.concatenate(held + [own], axis=0).astype(jnp.bfloat16)
    return running.reshape(-1, *final_state.shape[1:])[1:], window


def per_device(
    conv_in,
    gate_in,
    q_proj,
    k_proj,
    v_proj,
    conv_weight,
    conv_bias,
    proj_dt_weight,
    proj_bc_weight,
    dt_gain,
    dt_weight,
    dt_bias,
    decay_rate,
    skip_weight,
):
    tokens_here, channels = conv_in.shape
    key_span = WINDOW // tokens_here
    conv_tail = conv_in[tokens_here - (KCONV - 1) :]
    tail_in = shifted(conv_tail, "seq", 1)
    padded = jnp.concatenate([tail_in, conv_in], axis=0).astype(jnp.float32)
    activated = causal_conv(padded, conv_weight, conv_bias, tokens_here)
    state_parts = lax.dot_general(
        proj_bc_weight, activated, (((1,), (1,)), ((), ())), preferred_element_type=jnp.float32
    )
    rank_part = jnp.dot(activated, proj_dt_weight, preferred_element_type=jnp.float32)
    rank_width = rank_part.shape[1]
    packed = jnp.concatenate([rank_part, state_parts.reshape(-1, rank_width)], axis=0)
    total = butterfly_sum(packed, "tp")
    rank_low = total[:tokens_here]
    state_in = total[tokens_here:].reshape(state_parts.shape)
    rank_normed = rank_norm(rank_low, dt_gain)
    step_size = jax.nn.softplus(
        jnp.dot(rank_normed, dt_weight, preferred_element_type=jnp.float32) + dt_bias[None, :]
    )
    drive_term = step_size * activated.astype(jnp.float32)
    state_count = decay_rate.shape[0]
    lanes = channels // SUBLANES
    dt3 = step_size.reshape(tokens_here, SUBLANES, lanes)
    dr3 = drive_term.reshape(tokens_here, SUBLANES, lanes)
    rate3 = decay_rate.reshape(state_count, SUBLANES, lanes)
    zero_state = jnp.zeros((state_count, SUBLANES, lanes), jnp.float32)
    local_final = run_scan(state_in, dt3, dr3, rate3, zero_state, False)
    step_sum = jnp.sum(dt3, axis=0)
    own_kv = jnp.concatenate([k_proj, v_proj], axis=1)
    entering, window = scan_with_window(step_sum, local_final, rate3, own_kv, key_span)
    mamba_sum = run_scan(state_in, dt3, dr3, rate3, entering, True).reshape(tokens_here, channels)
    mamba_out = (
        (mamba_sum + skip_weight[None, :] * activated.astype(jnp.float32))
        * jax.nn.silu(gate_in.astype(jnp.float32))
    ).astype(jnp.bfloat16)
    base = (lax.axis_index("seq") * tokens_here).astype(jnp.int32).reshape(1)
    attn_out = run_attention(q_proj, window, base)
    return (mamba_out, attn_out)


def solution(mesh):
    return jax.shard_map(
        per_device,
        mesh=mesh,
        in_specs=(
            P("seq", "tp"),
            P("seq", "tp"),
            P("seq", "tp"),
            P("seq", "tp"),
            P("seq", "tp"),
            P(None, "tp"),
            P("tp"),
            P("tp", None),
            P(None, "tp"),
            P(),
            P(None, "tp"),
            P("tp"),
            P(None, "tp"),
            P("tp"),
        ),
        out_specs=(P("seq", "tp"), P("seq", "tp")),
        check_vma=False,
    )
```

```python
import functools
import math

import jax
import jax.numpy as jnp
from jax import lax
from jax.experimental import pallas as pl
from jax.experimental.pallas import tpu as pltpu
from jax.sharding import PartitionSpec as P

KCONV = 4
HD = 128
WINDOW = 2048
SUBLANES = 8
LANE_BLOCK = 128
epsilon = 1e-06


def shifted(value, axis, steps):
    count = lax.axis_size(axis)
    first, last = (max(0, -steps), min(count, count - steps))
    return lax.ppermute(value, axis, [(source, source + steps) for source in range(first, last)])


def causal_conv(padded, conv_weight, conv_bias, length):
    summed = conv_bias[None, :] + jnp.zeros((length, padded.shape[1]), jnp.float32)
    for offset in range(KCONV):
        summed = summed + conv_weight[offset][None, :] * padded[offset : offset + length]
    return jax.nn.silu(summed).astype(jnp.bfloat16)


def rank_norm(rank_low, dt_gain):
    mean_square = jnp.mean(rank_low * rank_low, axis=-1, keepdims=True)
    return (rank_low * lax.rsqrt(mean_square + epsilon) * dt_gain[None, :]).astype(jnp.bfloat16)


def scan_kernel(with_out, bc_ref, dt_ref, dr_ref, rate_ref, h0_ref, out_ref):
    states = rate_ref.shape[0]
    tokens = dt_ref.shape[0]
    neg_rate = [-rate_ref[n] for n in range(states)]

    def body(t, hs):
        dt = dt_ref[t]
        dr = dr_ref[t]
        new = []
        acc = None
        for n in range(states):
            h = jnp.exp(neg_rate[n] * dt) * hs[n] + bc_ref[n, t] * dr
            new.append(h)
            if with_out:
                term = bc_ref[states + n, t] * h
                acc = term if acc is None else acc + term
        if with_out:
            out_ref[t] = acc
        return tuple(new)

    hs = lax.fori_loop(0, tokens, body, tuple(h0_ref[n] for n in range(states)), unroll=2)
    if not with_out:
        for n in range(states):
            out_ref[n] = hs[n]


def run_scan(bc, dt3, dr3, rate3, h0, with_out):
    tokens, sub, lanes = dt3.shape
    states = rate3.shape[0]
    blocks = lanes // LANE_BLOCK
    row_spec = pl.BlockSpec((tokens, sub, LANE_BLOCK), lambda j: (0, 0, j))
    state_spec = pl.BlockSpec((states, sub, LANE_BLOCK), lambda j: (0, 0, j))
    out_shape = (tokens, sub, lanes) if with_out else (states, sub, lanes)
    elems = tokens * states * sub * lanes
    return pl.pallas_call(
        functools.partial(scan_kernel, with_out),
        grid=(blocks,),
        in_specs=[
            pl.BlockSpec(memory_space=pltpu.SMEM),
            row_spec,
            row_spec,
            state_spec,
            state_spec,
        ],
        out_specs=row_spec if with_out else state_spec,
        out_shape=jax.ShapeDtypeStruct(out_shape, jnp.float32),
        cost_estimate=pl.CostEstimate(
            flops=(6 if with_out else 4) * elems,
            transcendentals=elems,
            bytes_accessed=4 * (3 * tokens * sub * lanes + 2 * states * sub * lanes),
        ),
    )(bc, dt3, dr3, rate3, h0)


def attention_kernel(base_ref, q_ref, k_ref, v_ref, o_ref, bias_ref):
    @pl.when(pl.program_id(0) == 0)
    def _():
        rows = lax.broadcasted_iota(jnp.int32, bias_ref.shape, 0)
        cols = lax.broadcasted_iota(jnp.int32, bias_ref.shape, 1)
        distance = WINDOW + rows - cols
        in_window = (distance >= 0) & (distance < WINDOW) & (cols + base_ref[0] >= WINDOW)
        bias_ref[...] = jnp.where(in_window, 0.0, -jnp.inf)

    scores = lax.dot_general(
        q_ref[...], k_ref[...], (((1,), (1,)), ((), ())), preferred_element_type=jnp.float32
    ) * (1.0 / math.sqrt(HD)) + bias_ref[...]
    row_peak = jnp.max(scores, axis=1, keepdims=True)
    weights = jnp.exp(scores - row_peak).astype(jnp.bfloat16)
    summed = jnp.sum(weights.astype(jnp.float32), axis=1, keepdims=True)
    weighted = jnp.dot(weights, v_ref[...], preferred_element_type=jnp.float32)
    o_ref[...] = (weighted / summed).astype(o_ref.dtype)


def run_attention(q_proj, window, base):
    tokens, width = q_proj.shape
    keys = window.shape[0]
    heads = width // HD
    group = heads // (window.shape[1] // (2 * HD))
    return pl.pallas_call(
        attention_kernel,
        grid=(heads,),
        in_specs=[
            pl.BlockSpec(memory_space=pltpu.SMEM),
            pl.BlockSpec((tokens, HD), lambda h: (0, h)),
            pl.BlockSpec((keys, HD), lambda h: (0, h // group)),
            pl.BlockSpec((keys, HD), lambda h: (0, window.shape[1] // (2 * HD) + h // group)),
        ],
        out_specs=pl.BlockSpec((tokens, HD), lambda h: (0, h)),
        out_shape=jax.ShapeDtypeStruct((tokens, width), q_proj.dtype),
        scratch_shapes=[pltpu.VMEM((tokens, keys), jnp.float32)],
        cost_estimate=pl.CostEstimate(
            flops=4 * tokens * keys * HD * heads,
            transcendentals=tokens * keys * heads,
            bytes_accessed=2 * (2 * tokens * width + 2 * keys * window.shape[1]),
        ),
    )(base, q_proj, window, window)


def butterfly_sum(value, axis, first, last):
    stride = first
    while stride < last:
        pairs = [(source, source ^ stride) for source in range(lax.axis_size(axis))]
        value = value + lax.ppermute(value, axis, pairs)
        stride *= 2
    return value


def chip_first_sum(value, axis):
    count = lax.axis_size(axis)
    value = butterfly_sum(value, axis, 1, 2)
    half = value.shape[0] // 2
    core = lax.axis_index(axis) % 2
    mine = jnp.where(core == 0, value[:half], value[half:])
    mine = butterfly_sum(mine, axis, 2, count)
    other = lax.ppermute(mine, axis, [(source, source ^ 1) for source in range(count)])
    return jnp.where(core == 0, jnp.concatenate([mine, other]), jnp.concatenate([other, mine]))


def compose(earlier, later, rate3):
    decay = jnp.exp(-rate3 * later[0][None])
    states = decay * earlier[1:] + later[1:]
    return jnp.concatenate([(earlier[0] + later[0])[None], states], axis=0)


def entering_state(step_sum, final_state, rate3):
    local = jnp.concatenate([step_sum[None], final_state], axis=0)
    peers = lax.axis_size("seq")
    running = shifted(local, "seq", 1)
    distance = 1
    while distance < peers - 1:
        running = compose(shifted(running, "seq", distance), running, rate3)
        distance *= 2
    return running[1:]


def window_blocks(k_proj, v_proj, conv_tail, key_span):
    tokens = k_proj.shape[0]
    own = jnp.concatenate([k_proj, v_proj], axis=1)
    width = own.shape[1]
    tail = conv_tail.reshape(-1, width)
    first = shifted(jnp.concatenate([own, tail], axis=0), "seq", 1)
    tail_in = first[tokens:].reshape(conv_tail.shape)
    held = [first[:tokens], own]
    reach = 2
    while reach * 2 <= key_span:
        held = [shifted(jnp.concatenate(held, axis=0), "seq", reach)] + held
        reach *= 2
    assert reach == key_span
    held = [shifted(own, "seq", key_span)] + held
    return jnp.concatenate(held, axis=0), tail_in


def per_device(
    conv_in,
    gate_in,
    q_proj,
    k_proj,
    v_proj,
    conv_weight,
    conv_bias,
    proj_dt_weight,
    proj_bc_weight,
    dt_gain,
    dt_weight,
    dt_bias,
    decay_rate,
    skip_weight,
):
    tokens_here, channels = conv_in.shape
    key_span = WINDOW // tokens_here
    conv_tail = conv_in[tokens_here - (KCONV - 1) :]
    window, tail_in = window_blocks(k_proj, v_proj, conv_tail, key_span)
    padded = jnp.concatenate([tail_in, conv_in], axis=0).astype(jnp.float32)
    activated = causal_conv(padded, conv_weight, conv_bias, tokens_here)
    state_parts = lax.dot_general(
        proj_bc_weight, activated, (((1,), (1,)), ((), ())), preferred_element_type=jnp.float32
    )
    rank_part = jnp.dot(activated, proj_dt_weight, preferred_element_type=jnp.float32)
    rank_width = rank_part.shape[1]
    packed = jnp.concatenate([rank_part, state_parts.reshape(-1, rank_width)], axis=0)
    total = chip_first_sum(packed, "tp")
    rank_low = total[:tokens_here]
    state_in = total[tokens_here:].reshape(state_parts.shape)
    rank_normed = rank_norm(rank_low, dt_gain)
    step_size = jax.nn.softplus(
        jnp.dot(rank_normed, dt_weight, preferred_element_type=jnp.float32) + dt_bias[None, :]
    )
    drive_term = step_size * activated.astype(jnp.float32)
    state_count = decay_rate.shape[0]
    lanes = channels // SUBLANES
    dt3 = step_size.reshape(tokens_here, SUBLANES, lanes)
    dr3 = drive_term.reshape(tokens_here, SUBLANES, lanes)
    rate3 = decay_rate.reshape(state_count, SUBLANES, lanes)
    zero_state = jnp.zeros((state_count, SUBLANES, lanes), jnp.float32)
    local_final = run_scan(state_in, dt3, dr3, rate3, zero_state, False)
    step_sum = jnp.sum(dt3, axis=0)
    entering = entering_state(step_sum, local_final, rate3)
    mamba_sum = run_scan(state_in, dt3, dr3, rate3, entering, True).reshape(tokens_here, channels)
    mamba_out = (
        (mamba_sum + skip_weight[None, :] * activated.astype(jnp.float32))
        * jax.nn.silu(gate_in.astype(jnp.float32))
    ).astype(jnp.bfloat16)
    base = (lax.axis_index("seq") * tokens_here).astype(jnp.int32).reshape(1)
    attn_out = run_attention(q_proj, window, base)
    return (mamba_out, attn_out)


def solution(mesh):
    return jax.shard_map(
        per_device,
        mesh=mesh,
        in_specs=(
            P("seq", "tp"),
            P("seq", "tp"),
            P("seq", "tp"),
            P("seq", "tp"),
            P("seq", "tp"),
            P(None, "tp"),
            P("tp"),
            P("tp", None),
            P(None, "tp"),
            P(),
            P(None, "tp"),
            P("tp"),
            P(None, "tp"),
            P("tp"),
        ),
        out_specs=(P("seq", "tp"), P("seq", "tp")),
        check_vma=False,
    )
```

```python
import functools
import math

import jax
import jax.numpy as jnp
from jax import lax
from jax.experimental import pallas as pl
from jax.experimental.pallas import tpu as pltpu
from jax.sharding import PartitionSpec as P

KCONV = 4
HD = 128
WINDOW = 2048
SUBLANES = 8
LANE_BLOCK = 128
epsilon = 1e-06


def shifted(value, axis, steps):
    count = lax.axis_size(axis)
    first, last = (max(0, -steps), min(count, count - steps))
    return lax.ppermute(value, axis, [(source, source + steps) for source in range(first, last)])


def causal_conv(padded, conv_weight, conv_bias, length):
    summed = conv_bias[None, :] + jnp.zeros((length, padded.shape[1]), jnp.float32)
    for offset in range(KCONV):
        summed = summed + conv_weight[offset][None, :] * padded[offset : offset + length]
    return jax.nn.silu(summed).astype(jnp.bfloat16)


def rank_norm(rank_low, dt_gain):
    mean_square = jnp.mean(rank_low * rank_low, axis=-1, keepdims=True)
    return (rank_low * lax.rsqrt(mean_square + epsilon) * dt_gain[None, :]).astype(jnp.bfloat16)


def scan_kernel(with_out, bc_ref, dt_ref, dr_ref, rate_ref, h0_ref, out_ref):
    states = rate_ref.shape[0]
    tokens = dt_ref.shape[0]
    neg_rate = [-rate_ref[n] for n in range(states)]

    def body(t, hs):
        dt = dt_ref[t]
        dr = dr_ref[t]
        new = []
        acc = None
        for n in range(states):
            h = jnp.exp(neg_rate[n] * dt) * hs[n] + bc_ref[n, t] * dr
            new.append(h)
            if with_out:
                term = bc_ref[states + n, t] * h
                acc = term if acc is None else acc + term
        if with_out:
            out_ref[t] = acc
        return tuple(new)

    hs = lax.fori_loop(0, tokens, body, tuple(h0_ref[n] for n in range(states)), unroll=2)
    if not with_out:
        for n in range(states):
            out_ref[n] = hs[n]


def run_scan(bc, dt3, dr3, rate3, h0, with_out):
    tokens, sub, lanes = dt3.shape
    states = rate3.shape[0]
    blocks = lanes // LANE_BLOCK
    row_spec = pl.BlockSpec((tokens, sub, LANE_BLOCK), lambda j: (0, 0, j))
    state_spec = pl.BlockSpec((states, sub, LANE_BLOCK), lambda j: (0, 0, j))
    out_shape = (tokens, sub, lanes) if with_out else (states, sub, lanes)
    elems = tokens * states * sub * lanes
    return pl.pallas_call(
        functools.partial(scan_kernel, with_out),
        grid=(blocks,),
        in_specs=[
            pl.BlockSpec(memory_space=pltpu.SMEM),
            row_spec,
            row_spec,
            state_spec,
            state_spec,
        ],
        out_specs=row_spec if with_out else state_spec,
        out_shape=jax.ShapeDtypeStruct(out_shape, jnp.float32),
        cost_estimate=pl.CostEstimate(
            flops=(6 if with_out else 4) * elems,
            transcendentals=elems,
            bytes_accessed=4 * (3 * tokens * sub * lanes + 2 * states * sub * lanes),
        ),
    )(bc, dt3, dr3, rate3, h0)


def attention_kernel(base_ref, q_ref, k_ref, v_ref, o_ref, bias_ref):
    @pl.when(pl.program_id(0) == 0)
    def _():
        rows = lax.broadcasted_iota(jnp.int32, bias_ref.shape, 0)
        cols = lax.broadcasted_iota(jnp.int32, bias_ref.shape, 1)
        distance = WINDOW + rows - cols
        in_window = (distance >= 0) & (distance < WINDOW) & (cols + base_ref[0] >= WINDOW)
        bias_ref[...] = jnp.where(in_window, 0.0, -jnp.inf)

    scores = lax.dot_general(
        q_ref[...], k_ref[...], (((1,), (1,)), ((), ())), preferred_element_type=jnp.float32
    ) * (1.0 / math.sqrt(HD)) + bias_ref[...]
    row_peak = jnp.max(scores, axis=1, keepdims=True)
    weights = jnp.exp(scores - row_peak).astype(jnp.bfloat16)
    summed = jnp.sum(weights.astype(jnp.float32), axis=1, keepdims=True)
    weighted = jnp.dot(weights, v_ref[...], preferred_element_type=jnp.float32)
    o_ref[...] = (weighted / summed).astype(o_ref.dtype)


def run_attention(q_proj, window, base):
    tokens, width = q_proj.shape
    keys = window.shape[0]
    heads = width // HD
    group = heads // (window.shape[1] // (2 * HD))
    return pl.pallas_call(
        attention_kernel,
        grid=(heads,),
        in_specs=[
            pl.BlockSpec(memory_space=pltpu.SMEM),
            pl.BlockSpec((tokens, HD), lambda h: (0, h)),
            pl.BlockSpec((keys, HD), lambda h: (0, h // group)),
            pl.BlockSpec((keys, HD), lambda h: (0, window.shape[1] // (2 * HD) + h // group)),
        ],
        out_specs=pl.BlockSpec((tokens, HD), lambda h: (0, h)),
        out_shape=jax.ShapeDtypeStruct((tokens, width), q_proj.dtype),
        scratch_shapes=[pltpu.VMEM((tokens, keys), jnp.float32)],
        cost_estimate=pl.CostEstimate(
            flops=4 * tokens * keys * HD * heads,
            transcendentals=tokens * keys * heads,
            bytes_accessed=2 * (2 * tokens * width + 2 * keys * window.shape[1]),
        ),
    )(base, q_proj, window, window)


def butterfly_sum(value, axis, first, last):
    stride = first
    while stride < last:
        pairs = [(source, source ^ stride) for source in range(lax.axis_size(axis))]
        value = value + lax.ppermute(value, axis, pairs)
        stride *= 2
    return value


def chip_first_sum(value, axis, attend):
    count = lax.axis_size(axis)
    value = butterfly_sum(value, axis, 1, 2)
    half = value.shape[0] // 2
    core = lax.axis_index(axis) % 2
    mine = jnp.where(core == 0, value[:half], value[half:])
    mine = butterfly_sum(mine, axis, 2, 4)
    mine, attended = attend(mine)
    mine = butterfly_sum(mine, axis, 4, count)
    mine, attended = lax.optimization_barrier((mine, attended))
    other = lax.ppermute(mine, axis, [(source, source ^ 1) for source in range(count)])
    both = jnp.where(core == 0, jnp.concatenate([mine, other]), jnp.concatenate([other, mine]))
    return both, attended


def compose(earlier, later, rate3):
    decay = jnp.exp(-rate3 * later[0][None])
    states = decay * earlier[1:] + later[1:]
    return jnp.concatenate([(earlier[0] + later[0])[None], states], axis=0)


def entering_state(step_sum, final_state, rate3):
    local = jnp.concatenate([step_sum[None], final_state], axis=0)
    peers = lax.axis_size("seq")
    running = shifted(local, "seq", 1)
    distance = 1
    while distance < peers - 1:
        running = compose(shifted(running, "seq", distance), running, rate3)
        distance *= 2
    return running[1:]


def window_blocks(k_proj, v_proj, conv_tail, key_span):
    tokens = k_proj.shape[0]
    own = jnp.concatenate([k_proj, v_proj], axis=1)
    width = own.shape[1]
    tail = conv_tail.reshape(-1, width)
    first = shifted(jnp.concatenate([own, tail], axis=0), "seq", 1)
    tail_in = first[tokens:].reshape(conv_tail.shape)
    held = [first[:tokens], own]
    reach = 2
    while reach * 2 <= key_span:
        held = [shifted(jnp.concatenate(held, axis=0), "seq", reach)] + held
        reach *= 2
    assert reach == key_span
    held = [shifted(own, "seq", key_span)] + held
    return jnp.concatenate(held, axis=0), tail_in


def per_device(
    conv_in,
    gate_in,
    q_proj,
    k_proj,
    v_proj,
    conv_weight,
    conv_bias,
    proj_dt_weight,
    proj_bc_weight,
    dt_gain,
    dt_weight,
    dt_bias,
    decay_rate,
    skip_weight,
):
    tokens_here, channels = conv_in.shape
    key_span = WINDOW // tokens_here
    conv_tail = conv_in[tokens_here - (KCONV - 1) :]
    window, tail_in = window_blocks(k_proj, v_proj, conv_tail, key_span)
    padded = jnp.concatenate([tail_in, conv_in], axis=0).astype(jnp.float32)
    activated = causal_conv(padded, conv_weight, conv_bias, tokens_here)
    state_parts = lax.dot_general(
        proj_bc_weight, activated, (((1,), (1,)), ((), ())), preferred_element_type=jnp.float32
    )
    rank_part = jnp.dot(activated, proj_dt_weight, preferred_element_type=jnp.float32)
    rank_width = rank_part.shape[1]
    packed = jnp.concatenate([rank_part, state_parts.reshape(-1, rank_width)], axis=0)
    base = (lax.axis_index("seq") * tokens_here).astype(jnp.int32).reshape(1)

    def attend(partial):
        partial, ready = lax.optimization_barrier((partial, window))
        return partial, run_attention(q_proj, ready, base)

    total, attn_out = chip_first_sum(packed, "tp", attend)
    rank_low = total[:tokens_here]
    state_in = total[tokens_here:].reshape(state_parts.shape)
    rank_normed = rank_norm(rank_low, dt_gain)
    step_size = jax.nn.softplus(
        jnp.dot(rank_normed, dt_weight, preferred_element_type=jnp.float32) + dt_bias[None, :]
    )
    drive_term = step_size * activated.astype(jnp.float32)
    state_count = decay_rate.shape[0]
    lanes = channels // SUBLANES
    dt3 = step_size.reshape(tokens_here, SUBLANES, lanes)
    dr3 = drive_term.reshape(tokens_here, SUBLANES, lanes)
    rate3 = decay_rate.reshape(state_count, SUBLANES, lanes)
    zero_state = jnp.zeros((state_count, SUBLANES, lanes), jnp.float32)
    local_final = run_scan(state_in, dt3, dr3, rate3, zero_state, False)
    step_sum = jnp.sum(dt3, axis=0)
    entering = entering_state(step_sum, local_final, rate3)
    mamba_sum = run_scan(state_in, dt3, dr3, rate3, entering, True).reshape(tokens_here, channels)
    mamba_out = (
        (mamba_sum + skip_weight[None, :] * activated.astype(jnp.float32))
        * jax.nn.silu(gate_in.astype(jnp.float32))
    ).astype(jnp.bfloat16)
    return (mamba_out, attn_out)


def solution(mesh):
    return jax.shard_map(
        per_device,
        mesh=mesh,
        in_specs=(
            P("seq", "tp"),
            P("seq", "tp"),
            P("seq", "tp"),
            P("seq", "tp"),
            P("seq", "tp"),
            P(None, "tp"),
            P("tp"),
            P("tp", None),
            P(None, "tp"),
            P(),
            P(None, "tp"),
            P("tp"),
            P(None, "tp"),
            P("tp"),
        ),
        out_specs=(P("seq", "tp"), P("seq", "tp")),
        check_vma=False,
    )
```

```python
import functools
import math

import jax
import jax.numpy as jnp
from jax import lax
from jax.experimental import pallas as pl
from jax.experimental.pallas import tpu as pltpu
from jax.sharding import PartitionSpec as P

KCONV = 4
HD = 128
WINDOW = 2048
SUBLANES = 8
LANE_BLOCK = 128
epsilon = 1e-06


def shifted(value, axis, steps):
    count = lax.axis_size(axis)
    first, last = (max(0, -steps), min(count, count - steps))
    return lax.ppermute(value, axis, [(source, source + steps) for source in range(first, last)])


def causal_conv(padded, conv_weight, conv_bias, length):
    summed = conv_bias[None, :] + jnp.zeros((length, padded.shape[1]), jnp.float32)
    for offset in range(KCONV):
        summed = summed + conv_weight[offset][None, :] * padded[offset : offset + length]
    return jax.nn.silu(summed).astype(jnp.bfloat16)


def rank_norm(rank_low, dt_gain):
    mean_square = jnp.mean(rank_low * rank_low, axis=-1, keepdims=True)
    return (rank_low * lax.rsqrt(mean_square + epsilon) * dt_gain[None, :]).astype(jnp.bfloat16)


def scan_kernel(with_out, bc_ref, dt_ref, dr_ref, rate_ref, h0_ref, out_ref):
    states = rate_ref.shape[0]
    tokens = dt_ref.shape[0]
    neg_rate = [-rate_ref[n] for n in range(states)]

    def body(t, hs):
        dt = dt_ref[t]
        dr = dr_ref[t]
        new = []
        acc = None
        for n in range(states):
            h = jnp.exp(neg_rate[n] * dt) * hs[n] + bc_ref[n, t] * dr
            new.append(h)
            if with_out:
                term = bc_ref[states + n, t] * h
                acc = term if acc is None else acc + term
        if with_out:
            out_ref[t] = acc
        return tuple(new)

    hs = lax.fori_loop(0, tokens, body, tuple(h0_ref[n] for n in range(states)), unroll=2)
    if not with_out:
        for n in range(states):
            out_ref[n] = hs[n]


def run_scan(bc, dt3, dr3, rate3, h0, with_out):
    tokens, sub, lanes = dt3.shape
    states = rate3.shape[0]
    blocks = lanes // LANE_BLOCK
    row_spec = pl.BlockSpec((tokens, sub, LANE_BLOCK), lambda j: (0, 0, j))
    state_spec = pl.BlockSpec((states, sub, LANE_BLOCK), lambda j: (0, 0, j))
    out_shape = (tokens, sub, lanes) if with_out else (states, sub, lanes)
    elems = tokens * states * sub * lanes
    return pl.pallas_call(
        functools.partial(scan_kernel, with_out),
        grid=(blocks,),
        in_specs=[
            pl.BlockSpec(memory_space=pltpu.SMEM),
            row_spec,
            row_spec,
            state_spec,
            state_spec,
        ],
        out_specs=row_spec if with_out else state_spec,
        out_shape=jax.ShapeDtypeStruct(out_shape, jnp.float32),
        cost_estimate=pl.CostEstimate(
            flops=(6 if with_out else 4) * elems,
            transcendentals=elems,
            bytes_accessed=4 * (3 * tokens * sub * lanes + 2 * states * sub * lanes),
        ),
    )(bc, dt3, dr3, rate3, h0)


def attention_kernel(base_ref, q_ref, k_ref, v_ref, o_ref, bias_ref):
    @pl.when(pl.program_id(0) == 0)
    def _():
        rows = lax.broadcasted_iota(jnp.int32, bias_ref.shape, 0)
        cols = lax.broadcasted_iota(jnp.int32, bias_ref.shape, 1)
        distance = WINDOW + rows - cols
        in_window = (distance >= 0) & (distance < WINDOW) & (cols + base_ref[0] >= WINDOW)
        bias_ref[...] = jnp.where(in_window, 0.0, -jnp.inf)

    scores = lax.dot_general(
        q_ref[...], k_ref[...], (((1,), (1,)), ((), ())), preferred_element_type=jnp.float32
    ) * (1.0 / math.sqrt(HD)) + bias_ref[...]
    row_peak = jnp.max(scores, axis=1, keepdims=True)
    weights = jnp.exp(scores - row_peak).astype(jnp.bfloat16)
    summed = jnp.sum(weights.astype(jnp.float32), axis=1, keepdims=True)
    weighted = jnp.dot(weights, v_ref[...], preferred_element_type=jnp.float32)
    o_ref[...] = (weighted / summed).astype(o_ref.dtype)


def run_attention(q_proj, window, base):
    tokens, width = q_proj.shape
    keys = window.shape[0]
    heads = width // HD
    group = heads // (window.shape[1] // (2 * HD))
    return pl.pallas_call(
        attention_kernel,
        grid=(heads,),
        in_specs=[
            pl.BlockSpec(memory_space=pltpu.SMEM),
            pl.BlockSpec((tokens, HD), lambda h: (0, h)),
            pl.BlockSpec((keys, HD), lambda h: (0, h // group)),
            pl.BlockSpec((keys, HD), lambda h: (0, window.shape[1] // (2 * HD) + h // group)),
        ],
        out_specs=pl.BlockSpec((tokens, HD), lambda h: (0, h)),
        out_shape=jax.ShapeDtypeStruct((tokens, width), q_proj.dtype),
        scratch_shapes=[pltpu.VMEM((tokens, keys), jnp.float32)],
        cost_estimate=pl.CostEstimate(
            flops=4 * tokens * keys * HD * heads,
            transcendentals=tokens * keys * heads,
            bytes_accessed=2 * (2 * tokens * width + 2 * keys * window.shape[1]),
        ),
    )(base, q_proj, window, window)


def butterfly_sum(value, axis, first, last):
    stride = first
    while stride < last:
        pairs = [(source, source ^ stride) for source in range(lax.axis_size(axis))]
        value = value + lax.ppermute(value, axis, pairs)
        stride *= 2
    return value


def chip_first_sum(value, axis):
    count = lax.axis_size(axis)
    value = butterfly_sum(value, axis, 1, 2)
    half = value.shape[0] // 2
    core = lax.axis_index(axis) % 2
    mine = jnp.where(core == 0, value[:half], value[half:])
    mine = butterfly_sum(mine, axis, 2, count)
    other = lax.ppermute(mine, axis, [(source, source ^ 1) for source in range(count)])
    return jnp.where(core == 0, jnp.concatenate([mine, other]), jnp.concatenate([other, mine]))


def compose(earlier, later, rate3):
    decay = jnp.exp(-rate3 * later[0][None])
    states = decay * earlier[1:] + later[1:]
    return jnp.concatenate([(earlier[0] + later[0])[None], states], axis=0)


def entering_state(step_sum, final_state, rate3):
    inclusive = jnp.concatenate([step_sum[None], final_state], axis=0)
    exclusive = None
    peers = lax.axis_size("seq")
    distance = 1
    while distance < peers:
        received = shifted(inclusive, "seq", distance)
        exclusive = received if exclusive is None else compose(received, exclusive, rate3)
        if distance * 2 < peers:
            inclusive = compose(received, inclusive, rate3)
        distance *= 2
    return exclusive[1:]


def window_blocks(k_proj, v_proj, conv_tail, key_span):
    tokens = k_proj.shape[0]
    own = jnp.concatenate([k_proj, v_proj], axis=1)
    width = own.shape[1]
    tail = conv_tail.reshape(-1, width)
    first = shifted(jnp.concatenate([own, tail], axis=0), "seq", 1)
    tail_in = first[tokens:].reshape(conv_tail.shape)
    held = [first[:tokens], own]
    reach = 2
    while reach * 2 <= key_span:
        held = [shifted(jnp.concatenate(held, axis=0), "seq", reach)] + held
        reach *= 2
    assert reach == key_span
    held = [shifted(own, "seq", key_span)] + held
    return jnp.concatenate(held, axis=0), tail_in


def per_device(
    conv_in,
    gate_in,
    q_proj,
    k_proj,
    v_proj,
    conv_weight,
    conv_bias,
    proj_dt_weight,
    proj_bc_weight,
    dt_gain,
    dt_weight,
    dt_bias,
    decay_rate,
    skip_weight,
):
    tokens_here, channels = conv_in.shape
    key_span = WINDOW // tokens_here
    conv_tail = conv_in[tokens_here - (KCONV - 1) :]
    window, tail_in = window_blocks(k_proj, v_proj, conv_tail, key_span)
    padded = jnp.concatenate([tail_in, conv_in], axis=0).astype(jnp.float32)
    activated = causal_conv(padded, conv_weight, conv_bias, tokens_here)
    state_parts = lax.dot_general(
        proj_bc_weight, activated, (((1,), (1,)), ((), ())), preferred_element_type=jnp.float32
    )
    rank_part = jnp.dot(activated, proj_dt_weight, preferred_element_type=jnp.float32)
    rank_width = rank_part.shape[1]
    packed = jnp.concatenate([rank_part, state_parts.reshape(-1, rank_width)], axis=0)
    total = chip_first_sum(packed, "tp")
    rank_low = total[:tokens_here]
    state_in = total[tokens_here:].reshape(state_parts.shape)
    rank_normed = rank_norm(rank_low, dt_gain)
    step_size = jax.nn.softplus(
        jnp.dot(rank_normed, dt_weight, preferred_element_type=jnp.float32) + dt_bias[None, :]
    )
    drive_term = step_size * activated.astype(jnp.float32)
    state_count = decay_rate.shape[0]
    lanes = channels // SUBLANES
    dt3 = step_size.reshape(tokens_here, SUBLANES, lanes)
    dr3 = drive_term.reshape(tokens_here, SUBLANES, lanes)
    rate3 = decay_rate.reshape(state_count, SUBLANES, lanes)
    zero_state = jnp.zeros((state_count, SUBLANES, lanes), jnp.float32)
    local_final = run_scan(state_in, dt3, dr3, rate3, zero_state, False)
    step_sum = jnp.sum(dt3, axis=0)
    entering = entering_state(step_sum, local_final, rate3)
    mamba_sum = run_scan(state_in, dt3, dr3, rate3, entering, True).reshape(tokens_here, channels)
    mamba_out = (
        (mamba_sum + skip_weight[None, :] * activated.astype(jnp.float32))
        * jax.nn.silu(gate_in.astype(jnp.float32))
    ).astype(jnp.bfloat16)
    base = (lax.axis_index("seq") * tokens_here).astype(jnp.int32).reshape(1)
    attn_out = run_attention(q_proj, window, base)
    return (mamba_out, attn_out)


def solution(mesh):
    return jax.shard_map(
        per_device,
        mesh=mesh,
        in_specs=(
            P("seq", "tp"),
            P("seq", "tp"),
            P("seq", "tp"),
            P("seq", "tp"),
            P("seq", "tp"),
            P(None, "tp"),
            P("tp"),
            P("tp", None),
            P(None, "tp"),
            P(),
            P(None, "tp"),
            P("tp"),
            P(None, "tp"),
            P("tp"),
        ),
        out_specs=(P("seq", "tp"), P("seq", "tp")),
        check_vma=False,
    )
```

```python
import functools
import math

import jax
import jax.numpy as jnp
from jax import lax
from jax.experimental import pallas as pl
from jax.experimental.pallas import tpu as pltpu
from jax.sharding import PartitionSpec as P

KCONV = 4
HD = 128
WINDOW = 2048
SUBLANES = 8
LANE_BLOCK = 128
epsilon = 1e-06


def shifted(value, axis, steps):
    count = lax.axis_size(axis)
    first, last = (max(0, -steps), min(count, count - steps))
    return lax.ppermute(value, axis, [(source, source + steps) for source in range(first, last)])


def causal_conv(padded, conv_weight, conv_bias, length):
    summed = conv_bias[None, :] + jnp.zeros((length, padded.shape[1]), jnp.float32)
    for offset in range(KCONV):
        summed = summed + conv_weight[offset][None, :] * padded[offset : offset + length]
    return jax.nn.silu(summed).astype(jnp.bfloat16)


def rank_norm(rank_low, dt_gain):
    mean_square = jnp.mean(rank_low * rank_low, axis=-1, keepdims=True)
    return (rank_low * lax.rsqrt(mean_square + epsilon) * dt_gain[None, :]).astype(jnp.bfloat16)


def scan_kernel(with_out, bc_ref, dt_ref, dr_ref, rate_ref, h0_ref, out_ref):
    states = rate_ref.shape[0]
    tokens = dt_ref.shape[0]
    neg_rate = [-rate_ref[n] for n in range(states)]

    def body(t, hs):
        dt = dt_ref[t]
        dr = dr_ref[t]
        new = []
        acc = None
        for n in range(states):
            h = jnp.exp(neg_rate[n] * dt) * hs[n] + bc_ref[n, t] * dr
            new.append(h)
            if with_out:
                term = bc_ref[states + n, t] * h
                acc = term if acc is None else acc + term
        if with_out:
            out_ref[t] = acc
        return tuple(new)

    hs = lax.fori_loop(0, tokens, body, tuple(h0_ref[n] for n in range(states)), unroll=2)
    if not with_out:
        for n in range(states):
            out_ref[n] = hs[n]


def run_scan(bc, dt3, dr3, rate3, h0, with_out):
    tokens, sub, lanes = dt3.shape
    states = rate3.shape[0]
    blocks = lanes // LANE_BLOCK
    row_spec = pl.BlockSpec((tokens, sub, LANE_BLOCK), lambda j: (0, 0, j))
    state_spec = pl.BlockSpec((states, sub, LANE_BLOCK), lambda j: (0, 0, j))
    out_shape = (tokens, sub, lanes) if with_out else (states, sub, lanes)
    elems = tokens * states * sub * lanes
    return pl.pallas_call(
        functools.partial(scan_kernel, with_out),
        grid=(blocks,),
        in_specs=[
            pl.BlockSpec(memory_space=pltpu.SMEM),
            row_spec,
            row_spec,
            state_spec,
            state_spec,
        ],
        out_specs=row_spec if with_out else state_spec,
        out_shape=jax.ShapeDtypeStruct(out_shape, jnp.float32),
        cost_estimate=pl.CostEstimate(
            flops=(6 if with_out else 4) * elems,
            transcendentals=elems,
            bytes_accessed=4 * (3 * tokens * sub * lanes + 2 * states * sub * lanes),
        ),
    )(bc, dt3, dr3, rate3, h0)


def attention_kernel(base_ref, q_ref, k_ref, v_ref, o_ref, bias_ref):
    @pl.when(pl.program_id(0) == 0)
    def _():
        rows = lax.broadcasted_iota(jnp.int32, bias_ref.shape, 0)
        cols = lax.broadcasted_iota(jnp.int32, bias_ref.shape, 1)
        distance = WINDOW + rows - cols
        in_window = (distance >= 0) & (distance < WINDOW) & (cols + base_ref[0] >= WINDOW)
        bias_ref[...] = jnp.where(in_window, 0.0, -jnp.inf)

    scores = lax.dot_general(
        q_ref[...], k_ref[...], (((1,), (1,)), ((), ())), preferred_element_type=jnp.float32
    ) * (1.0 / math.sqrt(HD)) + bias_ref[...]
    row_peak = jnp.max(scores, axis=1, keepdims=True)
    weights = jnp.exp(scores - row_peak).astype(jnp.bfloat16)
    summed = jnp.sum(weights.astype(jnp.float32), axis=1, keepdims=True)
    weighted = jnp.dot(weights, v_ref[...], preferred_element_type=jnp.float32)
    o_ref[...] = (weighted / summed).astype(o_ref.dtype)


def run_attention(q_proj, window, base):
    tokens, width = q_proj.shape
    keys = window.shape[0]
    heads = width // HD
    group = heads // (window.shape[1] // (2 * HD))
    return pl.pallas_call(
        attention_kernel,
        grid=(heads,),
        in_specs=[
            pl.BlockSpec(memory_space=pltpu.SMEM),
            pl.BlockSpec((tokens, HD), lambda h: (0, h)),
            pl.BlockSpec((keys, HD), lambda h: (0, h // group)),
            pl.BlockSpec((keys, HD), lambda h: (0, window.shape[1] // (2 * HD) + h // group)),
        ],
        out_specs=pl.BlockSpec((tokens, HD), lambda h: (0, h)),
        out_shape=jax.ShapeDtypeStruct((tokens, width), q_proj.dtype),
        scratch_shapes=[pltpu.VMEM((tokens, keys), jnp.float32)],
        cost_estimate=pl.CostEstimate(
            flops=4 * tokens * keys * HD * heads,
            transcendentals=tokens * keys * heads,
            bytes_accessed=2 * (2 * tokens * width + 2 * keys * window.shape[1]),
        ),
    )(base, q_proj, window, window)


def butterfly_sum(value, axis, first, last):
    stride = first
    while stride < last:
        pairs = [(source, source ^ stride) for source in range(lax.axis_size(axis))]
        value = value + lax.ppermute(value, axis, pairs)
        stride *= 2
    return value


def chip_first_sum(value, axis):
    count = lax.axis_size(axis)
    value = butterfly_sum(value, axis, 1, 2)
    half = value.shape[0] // 2
    core = lax.axis_index(axis) % 2
    mine = jnp.where(core == 0, value[:half], value[half:])
    mine = butterfly_sum(mine, axis, 2, count)
    other = lax.ppermute(mine, axis, [(source, source ^ 1) for source in range(count)])
    return jnp.where(core == 0, jnp.concatenate([mine, other]), jnp.concatenate([other, mine]))


def compose(earlier, later, rate3):
    decay = jnp.exp(-rate3 * later[0][None])
    states = decay * earlier[1:] + later[1:]
    return jnp.concatenate([(earlier[0] + later[0])[None], states], axis=0)


def entering_state(step_sum, final_state, rate3):
    inclusive = jnp.concatenate([step_sum[None], final_state], axis=0)
    exclusive = None
    peers = lax.axis_size("seq")
    distance = 1
    while distance < peers:
        received = shifted(inclusive, "seq", distance)
        exclusive = received if exclusive is None else compose(received, exclusive, rate3)
        if distance * 2 < peers:
            inclusive = compose(received, inclusive, rate3)
        distance *= 2
    return exclusive[1:]


def window_blocks(k_proj, v_proj, conv_tail, key_span):
    tokens = k_proj.shape[0]
    own = jnp.concatenate([k_proj, v_proj], axis=1)
    width = own.shape[1]
    tail = conv_tail.reshape(-1, width)
    first = shifted(jnp.concatenate([own, tail], axis=0), "seq", 1)
    tail_in = first[tokens:].reshape(conv_tail.shape)
    held = [first[:tokens], own]
    reach = 2
    while reach * 2 <= key_span:
        held = [shifted(jnp.concatenate(held, axis=0), "seq", reach)] + held
        reach *= 2
    assert reach == key_span
    held = [shifted(own, "seq", key_span)] + held
    return jnp.concatenate(held, axis=0), tail_in


def per_device(
    conv_in,
    gate_in,
    q_proj,
    k_proj,
    v_proj,
    conv_weight,
    conv_bias,
    proj_dt_weight,
    proj_bc_weight,
    dt_gain,
    dt_weight,
    dt_bias,
    decay_rate,
    skip_weight,
):
    tokens_here, channels = conv_in.shape
    key_span = WINDOW // tokens_here
    conv_tail = conv_in[tokens_here - (KCONV - 1) :]
    window, tail_in = window_blocks(k_proj, v_proj, conv_tail, key_span)
    padded = jnp.concatenate([tail_in, conv_in], axis=0).astype(jnp.float32)
    activated = causal_conv(padded, conv_weight, conv_bias, tokens_here)
    state_parts = lax.dot_general(
        proj_bc_weight, activated, (((1,), (1,)), ((), ())), preferred_element_type=jnp.float32
    )
    rank_part = jnp.dot(activated, proj_dt_weight, preferred_element_type=jnp.float32)
    rank_width = rank_part.shape[1]
    packed = jnp.concatenate([rank_part, state_parts.reshape(-1, rank_width)], axis=0)
    total = chip_first_sum(packed, "tp")
    rank_low = total[:tokens_here]
    state_in = total[tokens_here:].reshape(state_parts.shape)
    rank_normed = rank_norm(rank_low, dt_gain)
    state_count = decay_rate.shape[0]
    lanes = channels // SUBLANES

    def cube(matrix):
        return matrix.reshape(matrix.shape[:-1] + (SUBLANES, lanes))

    act3 = cube(activated).astype(jnp.float32)
    dt3 = jax.nn.softplus(
        jnp.einsum("tr,rsl->tsl", rank_normed, cube(dt_weight), preferred_element_type=jnp.float32)
        + cube(dt_bias)[None]
    )
    dr3 = dt3 * act3
    rate3 = cube(decay_rate)
    zero_state = jnp.zeros((state_count, SUBLANES, lanes), jnp.float32)
    local_final = run_scan(state_in, dt3, dr3, rate3, zero_state, False)
    step_sum = jnp.sum(dt3, axis=0)
    entering = entering_state(step_sum, local_final, rate3)
    mamba_sum = run_scan(state_in, dt3, dr3, rate3, entering, True)
    mamba_out = (
        ((mamba_sum + cube(skip_weight)[None] * act3) * jax.nn.silu(cube(gate_in).astype(jnp.float32)))
        .astype(jnp.bfloat16)
        .reshape(tokens_here, channels)
    )
    base = (lax.axis_index("seq") * tokens_here).astype(jnp.int32).reshape(1)
    attn_out = run_attention(q_proj, window, base)
    return (mamba_out, attn_out)


def solution(mesh):
    return jax.shard_map(
        per_device,
        mesh=mesh,
        in_specs=(
            P("seq", "tp"),
            P("seq", "tp"),
            P("seq", "tp"),
            P("seq", "tp"),
            P("seq", "tp"),
            P(None, "tp"),
            P("tp"),
            P("tp", None),
            P(None, "tp"),
            P(),
            P(None, "tp"),
            P("tp"),
            P(None, "tp"),
            P("tp"),
        ),
        out_specs=(P("seq", "tp"), P("seq", "tp")),
        check_vma=False,
    )
```

```python
import functools
import math

import jax
import jax.numpy as jnp
from jax import lax
from jax.experimental import pallas as pl
from jax.experimental.pallas import tpu as pltpu
from jax.sharding import PartitionSpec as P

KCONV = 4
HD = 128
WINDOW = 2048
SUBLANES = 8
LANE_BLOCK = 128
epsilon = 1e-06


def shifted(value, axis, steps):
    count = lax.axis_size(axis)
    first, last = (max(0, -steps), min(count, count - steps))
    return lax.ppermute(value, axis, [(source, source + steps) for source in range(first, last)])


def causal_conv(padded, conv_weight, conv_bias, length):
    summed = conv_bias[None, :] + jnp.zeros((length, padded.shape[1]), jnp.float32)
    for offset in range(KCONV):
        summed = summed + conv_weight[offset][None, :] * padded[offset : offset + length]
    return jax.nn.silu(summed).astype(jnp.bfloat16)


def rank_norm(rank_low, dt_gain):
    mean_square = jnp.mean(rank_low * rank_low, axis=-1, keepdims=True)
    return (rank_low * lax.rsqrt(mean_square + epsilon) * dt_gain[None, :]).astype(jnp.bfloat16)


def scan_kernel(with_out, bc_ref, dt_ref, dr_ref, rate_ref, h0_ref, out_ref):
    states = rate_ref.shape[0]
    tokens = dt_ref.shape[0]
    neg_rate = [-rate_ref[n] for n in range(states)]

    def body(t, hs):
        dt = dt_ref[t]
        dr = dr_ref[t]
        new = []
        acc = None
        for n in range(states):
            h = jnp.exp(neg_rate[n] * dt) * hs[n] + bc_ref[n, t] * dr
            new.append(h)
            if with_out:
                term = bc_ref[states + n, t] * h
                acc = term if acc is None else acc + term
        if with_out:
            out_ref[t] = acc
        return tuple(new)

    hs = lax.fori_loop(0, tokens, body, tuple(h0_ref[n] for n in range(states)), unroll=2)
    if not with_out:
        for n in range(states):
            out_ref[n] = hs[n]


def run_scan(bc, dt3, dr3, rate3, h0, with_out):
    tokens, sub, lanes = dt3.shape
    states = rate3.shape[0]
    blocks = lanes // LANE_BLOCK
    row_spec = pl.BlockSpec((tokens, sub, LANE_BLOCK), lambda j: (0, 0, j))
    state_spec = pl.BlockSpec((states, sub, LANE_BLOCK), lambda j: (0, 0, j))
    out_shape = (tokens, sub, lanes) if with_out else (states, sub, lanes)
    elems = tokens * states * sub * lanes
    return pl.pallas_call(
        functools.partial(scan_kernel, with_out),
        grid=(blocks,),
        in_specs=[
            pl.BlockSpec(memory_space=pltpu.SMEM),
            row_spec,
            row_spec,
            state_spec,
            state_spec,
        ],
        out_specs=row_spec if with_out else state_spec,
        out_shape=jax.ShapeDtypeStruct(out_shape, jnp.float32),
        cost_estimate=pl.CostEstimate(
            flops=(6 if with_out else 4) * elems,
            transcendentals=elems,
            bytes_accessed=4 * (3 * tokens * sub * lanes + 2 * states * sub * lanes),
        ),
    )(bc, dt3, dr3, rate3, h0)


def attention_kernel(base_ref, q_ref, k_ref, v_ref, o_ref, bias_ref):
    @pl.when(pl.program_id(0) == 0)
    def _():
        rows = lax.broadcasted_iota(jnp.int32, bias_ref.shape, 0)
        cols = lax.broadcasted_iota(jnp.int32, bias_ref.shape, 1)
        distance = WINDOW + rows - cols
        in_window = (distance >= 0) & (distance < WINDOW) & (cols + base_ref[0] >= WINDOW)
        bias_ref[...] = jnp.where(in_window, 0.0, -jnp.inf)

    scores = lax.dot_general(
        q_ref[...], k_ref[...], (((1,), (1,)), ((), ())), preferred_element_type=jnp.float32
    ) * (1.0 / math.sqrt(HD)) + bias_ref[...]
    row_peak = jnp.max(scores, axis=1, keepdims=True)
    weights = jnp.exp(scores - row_peak).astype(jnp.bfloat16)
    ones = jnp.ones(v_ref.shape, v_ref.dtype)
    summed = jnp.dot(weights, ones, preferred_element_type=jnp.float32)
    weighted = jnp.dot(weights, v_ref[...], preferred_element_type=jnp.float32)
    o_ref[...] = (weighted / summed).astype(o_ref.dtype)


def run_attention(q_proj, window, base):
    tokens, width = q_proj.shape
    keys = window.shape[0]
    heads = width // HD
    group = heads // (window.shape[1] // (2 * HD))
    return pl.pallas_call(
        attention_kernel,
        grid=(heads,),
        in_specs=[
            pl.BlockSpec(memory_space=pltpu.SMEM),
            pl.BlockSpec((tokens, HD), lambda h: (0, h)),
            pl.BlockSpec((keys, HD), lambda h: (0, h // group)),
            pl.BlockSpec((keys, HD), lambda h: (0, window.shape[1] // (2 * HD) + h // group)),
        ],
        out_specs=pl.BlockSpec((tokens, HD), lambda h: (0, h)),
        out_shape=jax.ShapeDtypeStruct((tokens, width), q_proj.dtype),
        scratch_shapes=[pltpu.VMEM((tokens, keys), jnp.float32)],
        cost_estimate=pl.CostEstimate(
            flops=4 * tokens * keys * HD * heads,
            transcendentals=tokens * keys * heads,
            bytes_accessed=2 * (2 * tokens * width + 2 * keys * window.shape[1]),
        ),
    )(base, q_proj, window, window)


def butterfly_sum(value, axis, first, last):
    stride = first
    while stride < last:
        pairs = [(source, source ^ stride) for source in range(lax.axis_size(axis))]
        value = value + lax.ppermute(value, axis, pairs)
        stride *= 2
    return value


def chip_first_sum(value, axis):
    count = lax.axis_size(axis)
    value = butterfly_sum(value, axis, 1, 2)
    half = value.shape[0] // 2
    core = lax.axis_index(axis) % 2
    mine = jnp.where(core == 0, value[:half], value[half:])
    mine = butterfly_sum(mine, axis, 2, count)
    other = lax.ppermute(mine, axis, [(source, source ^ 1) for source in range(count)])
    return jnp.where(core == 0, jnp.concatenate([mine, other]), jnp.concatenate([other, mine]))


def compose(earlier, later, rate3):
    decay = jnp.exp(-rate3 * later[0][None])
    states = decay * earlier[1:] + later[1:]
    return jnp.concatenate([(earlier[0] + later[0])[None], states], axis=0)


def entering_state(step_sum, final_state, rate3):
    inclusive = jnp.concatenate([step_sum[None], final_state], axis=0)
    exclusive = None
    peers = lax.axis_size("seq")
    distance = 1
    while distance < peers:
        received = shifted(inclusive, "seq", distance)
        exclusive = received if exclusive is None else compose(received, exclusive, rate3)
        if distance * 2 < peers:
            inclusive = compose(received, inclusive, rate3)
        distance *= 2
    return exclusive[1:]


def window_blocks(k_proj, v_proj, conv_tail, key_span):
    tokens = k_proj.shape[0]
    own = jnp.concatenate([k_proj, v_proj], axis=1)
    width = own.shape[1]
    tail = conv_tail.reshape(-1, width)
    first = shifted(jnp.concatenate([own, tail], axis=0), "seq", 1)
    tail_in = first[tokens:].reshape(conv_tail.shape)
    held = [first[:tokens], own]
    reach = 2
    while reach * 2 <= key_span:
        held = [shifted(jnp.concatenate(held, axis=0), "seq", reach)] + held
        reach *= 2
    assert reach == key_span
    held = [shifted(own, "seq", key_span)] + held
    return jnp.concatenate(held, axis=0), tail_in


def per_device(
    conv_in,
    gate_in,
    q_proj,
    k_proj,
    v_proj,
    conv_weight,
    conv_bias,
    proj_dt_weight,
    proj_bc_weight,
    dt_gain,
    dt_weight,
    dt_bias,
    decay_rate,
    skip_weight,
):
    tokens_here, channels = conv_in.shape
    key_span = WINDOW // tokens_here
    conv_tail = conv_in[tokens_here - (KCONV - 1) :]
    window, tail_in = window_blocks(k_proj, v_proj, conv_tail, key_span)
    padded = jnp.concatenate([tail_in, conv_in], axis=0).astype(jnp.float32)
    activated = causal_conv(padded, conv_weight, conv_bias, tokens_here)
    state_parts = lax.dot_general(
        proj_bc_weight, activated, (((1,), (1,)), ((), ())), preferred_element_type=jnp.float32
    )
    rank_part = jnp.dot(activated, proj_dt_weight, preferred_element_type=jnp.float32)
    rank_width = rank_part.shape[1]
    packed = jnp.concatenate([rank_part, state_parts.reshape(-1, rank_width)], axis=0)
    lanes = channels // SUBLANES

    def cube(matrix):
        return matrix.reshape(matrix.shape[:-1] + (SUBLANES, lanes))

    act3 = cube(activated).astype(jnp.float32)
    gate3 = jax.nn.silu(cube(gate_in).astype(jnp.float32))
    total = chip_first_sum(packed, "tp")
    total, window, act3, gate3 = lax.optimization_barrier((total, window, act3, gate3))
    rank_low = total[:tokens_here]
    state_in = total[tokens_here:].reshape(state_parts.shape)
    rank_normed = rank_norm(rank_low, dt_gain)
    state_count = decay_rate.shape[0]
    dt3 = jax.nn.softplus(
        jnp.einsum("tr,rsl->tsl", rank_normed, cube(dt_weight), preferred_element_type=jnp.float32)
        + cube(dt_bias)[None]
    )
    dr3 = dt3 * act3
    rate3 = cube(decay_rate)
    zero_state = jnp.zeros((state_count, SUBLANES, lanes), jnp.float32)
    local_final = run_scan(state_in, dt3, dr3, rate3, zero_state, False)
    step_sum = jnp.sum(dt3, axis=0)
    entering = entering_state(step_sum, local_final, rate3)
    mamba_sum = run_scan(state_in, dt3, dr3, rate3, entering, True)
    mamba_out = (
        ((mamba_sum + cube(skip_weight)[None] * act3) * gate3)
        .astype(jnp.bfloat16)
        .reshape(tokens_here, channels)
    )
    base = (lax.axis_index("seq") * tokens_here).astype(jnp.int32).reshape(1)
    attn_out = run_attention(q_proj, window, base)
    return (mamba_out, attn_out)


def solution(mesh):
    return jax.shard_map(
        per_device,
        mesh=mesh,
        in_specs=(
            P("seq", "tp"),
            P("seq", "tp"),
            P("seq", "tp"),
            P("seq", "tp"),
            P("seq", "tp"),
            P(None, "tp"),
            P("tp"),
            P("tp", None),
            P(None, "tp"),
            P(),
            P(None, "tp"),
            P("tp"),
            P(None, "tp"),
            P("tp"),
        ),
        out_specs=(P("seq", "tp"), P("seq", "tp")),
        check_vma=False,
    )
```

```python
import functools
import math

import jax
import jax.numpy as jnp
from jax import lax
from jax.experimental import pallas as pl
from jax.experimental.pallas import tpu as pltpu
from jax.sharding import PartitionSpec as P

KCONV = 4
HD = 128
WINDOW = 2048
SUBLANES = 8
LANE_BLOCK = 128
epsilon = 1e-06


def shifted(value, axis, steps):
    count = lax.axis_size(axis)
    first, last = (max(0, -steps), min(count, count - steps))
    return lax.ppermute(value, axis, [(source, source + steps) for source in range(first, last)])


def causal_conv(padded, conv_weight, conv_bias, length):
    summed = conv_bias[None, :] + jnp.zeros((length, padded.shape[1]), jnp.float32)
    for offset in range(KCONV):
        summed = summed + conv_weight[offset][None, :] * padded[offset : offset + length]
    return jax.nn.silu(summed).astype(jnp.bfloat16)


def rank_norm(rank_low, dt_gain):
    mean_square = jnp.mean(rank_low * rank_low, axis=-1, keepdims=True)
    return (rank_low * lax.rsqrt(mean_square + epsilon) * dt_gain[None, :]).astype(jnp.bfloat16)


def scan_kernel(with_out, bc_ref, dt_ref, dr_ref, rate_ref, h0_ref, out_ref):
    states = rate_ref.shape[0]
    tokens = dt_ref.shape[0]
    neg_rate = [-rate_ref[n] for n in range(states)]

    def body(t, hs):
        dt = dt_ref[t]
        dr = dt * dr_ref[t]
        new = []
        acc = None
        for n in range(states):
            h = jnp.exp(neg_rate[n] * dt) * hs[n] + bc_ref[n, t] * dr
            new.append(h)
            if with_out:
                term = bc_ref[states + n, t] * h
                acc = term if acc is None else acc + term
        if with_out:
            out_ref[t] = acc
        return tuple(new)

    hs = lax.fori_loop(0, tokens, body, tuple(h0_ref[n] for n in range(states)), unroll=2)
    if not with_out:
        for n in range(states):
            out_ref[n] = hs[n]


def run_scan(bc, dt3, dr3, rate3, h0, with_out):
    tokens, sub, lanes = dt3.shape
    states = rate3.shape[0]
    blocks = lanes // LANE_BLOCK
    row_spec = pl.BlockSpec((tokens, sub, LANE_BLOCK), lambda j: (0, 0, j))
    state_spec = pl.BlockSpec((states, sub, LANE_BLOCK), lambda j: (0, 0, j))
    out_shape = (tokens, sub, lanes) if with_out else (states, sub, lanes)
    elems = tokens * states * sub * lanes
    return pl.pallas_call(
        functools.partial(scan_kernel, with_out),
        grid=(blocks,),
        in_specs=[
            pl.BlockSpec(memory_space=pltpu.SMEM),
            row_spec,
            row_spec,
            state_spec,
            state_spec,
        ],
        out_specs=row_spec if with_out else state_spec,
        out_shape=jax.ShapeDtypeStruct(out_shape, jnp.float32),
        cost_estimate=pl.CostEstimate(
            flops=(6 if with_out else 4) * elems,
            transcendentals=elems,
            bytes_accessed=4 * (3 * tokens * sub * lanes + 2 * states * sub * lanes),
        ),
    )(bc, dt3, dr3, rate3, h0)


def attention_kernel(base_ref, q_ref, k_ref, v_ref, o_ref, bias_ref):
    @pl.when(pl.program_id(0) == 0)
    def _():
        rows = lax.broadcasted_iota(jnp.int32, bias_ref.shape, 0)
        cols = lax.broadcasted_iota(jnp.int32, bias_ref.shape, 1)
        distance = WINDOW + rows - cols
        in_window = (distance >= 0) & (distance < WINDOW) & (cols + base_ref[0] >= WINDOW)
        bias_ref[...] = jnp.where(in_window, 0.0, -jnp.inf)

    scores = jnp.dot(
        q_ref[...], k_ref[...], preferred_element_type=jnp.float32
    ) * (1.0 / math.sqrt(HD)) + bias_ref[...]
    row_peak = jnp.max(scores, axis=1, keepdims=True)
    weights = jnp.exp(scores - row_peak).astype(jnp.bfloat16)
    summed = jnp.sum(weights.astype(jnp.float32), axis=1, keepdims=True)
    weighted = jnp.dot(weights, v_ref[...], preferred_element_type=jnp.float32)
    o_ref[...] = (weighted / summed).astype(o_ref.dtype)


def run_attention(q_proj, window, base):
    tokens, width = q_proj.shape
    keys = window.shape[0]
    heads = width // HD
    group = heads // (window.shape[1] // (2 * HD))
    return pl.pallas_call(
        attention_kernel,
        grid=(heads,),
        in_specs=[
            pl.BlockSpec(memory_space=pltpu.SMEM),
            pl.BlockSpec((tokens, HD), lambda h: (0, h)),
            pl.BlockSpec((HD, keys), lambda h: (h // group, 0)),
            pl.BlockSpec((keys, HD), lambda h: (0, window.shape[1] // (2 * HD) + h // group)),
        ],
        out_specs=pl.BlockSpec((tokens, HD), lambda h: (0, h)),
        out_shape=jax.ShapeDtypeStruct((tokens, width), q_proj.dtype),
        scratch_shapes=[pltpu.VMEM((tokens, keys), jnp.float32)],
        cost_estimate=pl.CostEstimate(
            flops=4 * tokens * keys * HD * heads,
            transcendentals=tokens * keys * heads,
            bytes_accessed=2 * (2 * tokens * width + 2 * keys * window.shape[1]),
        ),
    )(base, q_proj, window[:, : width // group].T, window)


def butterfly_sum(value, axis, first, last):
    stride = first
    while stride < last:
        pairs = [(source, source ^ stride) for source in range(lax.axis_size(axis))]
        value = value + lax.ppermute(value, axis, pairs)
        stride *= 2
    return value


def chip_first_sum(value, axis):
    count = lax.axis_size(axis)
    value = butterfly_sum(value, axis, 1, 2)
    half = value.shape[0] // 2
    core = lax.axis_index(axis) % 2
    mine = jnp.where(core == 0, value[:half], value[half:])
    mine = butterfly_sum(mine, axis, 2, count)
    other = lax.ppermute(mine, axis, [(source, source ^ 1) for source in range(count)])
    return jnp.where(core == 0, jnp.concatenate([mine, other]), jnp.concatenate([other, mine]))


def compose(earlier, later, rate3):
    decay = jnp.exp(-rate3 * later[0][None])
    states = decay * earlier[1:] + later[1:]
    return jnp.concatenate([(earlier[0] + later[0])[None], states], axis=0)


def entering_state(step_sum, final_state, rate3):
    inclusive = jnp.concatenate([step_sum[None], final_state], axis=0)
    exclusive = None
    peers = lax.axis_size("seq")
    distance = 1
    while distance < peers:
        received = shifted(inclusive, "seq", distance)
        exclusive = received if exclusive is None else compose(received, exclusive, rate3)
        if distance * 2 < peers:
            inclusive = compose(received, inclusive, rate3)
        distance *= 2
    return exclusive[1:]


def window_blocks(k_proj, v_proj, conv_tail, key_span):
    tokens = k_proj.shape[0]
    own = jnp.concatenate([k_proj, v_proj], axis=1)
    width = own.shape[1]
    tail = conv_tail.reshape(-1, width)
    first = shifted(jnp.concatenate([own, tail], axis=0), "seq", 1)
    tail_in = first[tokens:].reshape(conv_tail.shape)
    held = [first[:tokens], own]
    reach = 2
    while reach * 2 <= key_span:
        held = [shifted(jnp.concatenate(held, axis=0), "seq", reach)] + held
        reach *= 2
    assert reach == key_span
    held = [shifted(own, "seq", key_span)] + held
    return jnp.concatenate(held, axis=0), tail_in


def per_device(
    conv_in,
    gate_in,
    q_proj,
    k_proj,
    v_proj,
    conv_weight,
    conv_bias,
    proj_dt_weight,
    proj_bc_weight,
    dt_gain,
    dt_weight,
    dt_bias,
    decay_rate,
    skip_weight,
):
    tokens_here, channels = conv_in.shape
    key_span = WINDOW // tokens_here
    conv_tail = conv_in[tokens_here - (KCONV - 1) :]
    window, tail_in = window_blocks(k_proj, v_proj, conv_tail, key_span)
    padded = jnp.concatenate([tail_in, conv_in], axis=0).astype(jnp.float32)
    activated = causal_conv(padded, conv_weight, conv_bias, tokens_here)
    state_parts = lax.dot_general(
        proj_bc_weight, activated, (((1,), (1,)), ((), ())), preferred_element_type=jnp.float32
    )
    rank_part = jnp.dot(activated, proj_dt_weight, preferred_element_type=jnp.float32)
    rank_width = rank_part.shape[1]
    packed = jnp.concatenate([rank_part, state_parts.reshape(-1, rank_width)], axis=0)
    total = chip_first_sum(packed, "tp")
    rank_low = total[:tokens_here]
    state_in = total[tokens_here:].reshape(state_parts.shape)
    rank_normed = rank_norm(rank_low, dt_gain)
    state_count = decay_rate.shape[0]
    lanes = channels // SUBLANES

    def cube(matrix):
        return matrix.reshape(matrix.shape[:-1] + (SUBLANES, lanes))

    act3 = cube(activated).astype(jnp.float32)
    dt3 = jax.nn.softplus(
        jnp.einsum("tr,rsl->tsl", rank_normed, cube(dt_weight), preferred_element_type=jnp.float32)
        + cube(dt_bias)[None]
    )
    rate3 = cube(decay_rate)
    zero_state = jnp.zeros((state_count, SUBLANES, lanes), jnp.float32)
    local_final = run_scan(state_in, dt3, act3, rate3, zero_state, False)
    step_sum = jnp.sum(dt3, axis=0)
    entering = entering_state(step_sum, local_final, rate3)
    mamba_sum = run_scan(state_in, dt3, act3, rate3, entering, True)
    mamba_out = (
        ((mamba_sum + cube(skip_weight)[None] * act3) * jax.nn.silu(cube(gate_in).astype(jnp.float32)))
        .astype(jnp.bfloat16)
        .reshape(tokens_here, channels)
    )
    base = (lax.axis_index("seq") * tokens_here).astype(jnp.int32).reshape(1)
    attn_out = run_attention(q_proj, window, base)
    return (mamba_out, attn_out)


def solution(mesh):
    return jax.shard_map(
        per_device,
        mesh=mesh,
        in_specs=(
            P("seq", "tp"),
            P("seq", "tp"),
            P("seq", "tp"),
            P("seq", "tp"),
            P("seq", "tp"),
            P(None, "tp"),
            P("tp"),
            P("tp", None),
            P(None, "tp"),
            P(),
            P(None, "tp"),
            P("tp"),
            P(None, "tp"),
            P("tp"),
        ),
        out_specs=(P("seq", "tp"), P("seq", "tp")),
        check_vma=False,
    )
```

```python
import functools
import math

import jax
import jax.numpy as jnp
from jax import lax
from jax.experimental import pallas as pl
from jax.experimental.pallas import tpu as pltpu
from jax.sharding import PartitionSpec as P

KCONV = 4
HD = 128
WINDOW = 2048
SUBLANES = 8
LANE_BLOCK = 128
epsilon = 1e-06


def shifted(value, axis, steps):
    count = lax.axis_size(axis)
    first, last = (max(0, -steps), min(count, count - steps))
    return lax.ppermute(value, axis, [(source, source + steps) for source in range(first, last)])


def causal_conv(padded, conv_weight, conv_bias, length):
    summed = conv_bias[None, :] + jnp.zeros((length, padded.shape[1]), jnp.float32)
    for offset in range(KCONV):
        summed = summed + conv_weight[offset][None, :] * padded[offset : offset + length]
    return jax.nn.silu(summed).astype(jnp.bfloat16)


def rank_norm(rank_low, dt_gain):
    mean_square = jnp.mean(rank_low * rank_low, axis=-1, keepdims=True)
    return (rank_low * lax.rsqrt(mean_square + epsilon) * dt_gain[None, :]).astype(jnp.bfloat16)


def scan_kernel(with_out, bc_ref, dt_ref, dr_ref, rate_ref, h0_ref, out_ref):
    states = rate_ref.shape[0]
    tokens = dt_ref.shape[0]
    neg_rate = [-rate_ref[n] for n in range(states)]

    def body(t, hs):
        dt = dt_ref[t]
        dr = dr_ref[t]
        new = []
        acc = None
        for n in range(states):
            h = jnp.exp(neg_rate[n] * dt) * hs[n] + bc_ref[n, t] * dr
            new.append(h)
            if with_out:
                term = bc_ref[states + n, t] * h
                acc = term if acc is None else acc + term
        if with_out:
            out_ref[t] = acc
        return tuple(new)

    hs = lax.fori_loop(0, tokens, body, tuple(h0_ref[n] for n in range(states)), unroll=2)
    if not with_out:
        for n in range(states):
            out_ref[n] = hs[n]


def run_scan(bc, dt3, dr3, rate3, h0, with_out):
    tokens, sub, lanes = dt3.shape
    states = rate3.shape[0]
    blocks = lanes // LANE_BLOCK
    row_spec = pl.BlockSpec((tokens, sub, LANE_BLOCK), lambda j: (0, 0, j))
    state_spec = pl.BlockSpec((states, sub, LANE_BLOCK), lambda j: (0, 0, j))
    out_shape = (tokens, sub, lanes) if with_out else (states, sub, lanes)
    elems = tokens * states * sub * lanes
    return pl.pallas_call(
        functools.partial(scan_kernel, with_out),
        grid=(blocks,),
        in_specs=[
            pl.BlockSpec(memory_space=pltpu.SMEM),
            row_spec,
            row_spec,
            state_spec,
            state_spec,
        ],
        out_specs=row_spec if with_out else state_spec,
        out_shape=jax.ShapeDtypeStruct(out_shape, jnp.float32),
        cost_estimate=pl.CostEstimate(
            flops=(6 if with_out else 4) * elems,
            transcendentals=elems,
            bytes_accessed=4 * (3 * tokens * sub * lanes + 2 * states * sub * lanes),
        ),
    )(bc, dt3, dr3, rate3, h0)


def attention_kernel(base_ref, q_ref, k_ref, v_ref, o_ref, bias_ref):
    @pl.when(pl.program_id(0) == 0)
    def _():
        rows = lax.broadcasted_iota(jnp.int32, bias_ref.shape, 0)
        cols = lax.broadcasted_iota(jnp.int32, bias_ref.shape, 1)
        distance = WINDOW + rows - cols
        in_window = (distance >= 0) & (distance < WINDOW) & (cols + base_ref[0] >= WINDOW)
        bias_ref[...] = jnp.where(in_window, 0.0, -jnp.inf)

    scores = lax.dot_general(
        q_ref[...], k_ref[...], (((1,), (1,)), ((), ())), preferred_element_type=jnp.float32
    ) * (1.0 / math.sqrt(HD)) + bias_ref[...]
    row_peak = jnp.max(scores, axis=1, keepdims=True)
    weights = jnp.exp(scores - row_peak).astype(jnp.bfloat16)
    summed = jnp.sum(weights.astype(jnp.float32), axis=1, keepdims=True)
    weighted = jnp.dot(weights, v_ref[...], preferred_element_type=jnp.float32)
    o_ref[...] = (weighted / summed).astype(o_ref.dtype)


def run_attention(q_proj, window, base):
    tokens, width = q_proj.shape
    keys = window.shape[0]
    heads = width // HD
    group = heads // (window.shape[1] // (2 * HD))
    return pl.pallas_call(
        attention_kernel,
        grid=(heads,),
        in_specs=[
            pl.BlockSpec(memory_space=pltpu.SMEM),
            pl.BlockSpec((tokens, HD), lambda h: (0, h)),
            pl.BlockSpec((keys, HD), lambda h: (0, h // group)),
            pl.BlockSpec((keys, HD), lambda h: (0, window.shape[1] // (2 * HD) + h // group)),
        ],
        out_specs=pl.BlockSpec((tokens, HD), lambda h: (0, h)),
        out_shape=jax.ShapeDtypeStruct((tokens, width), q_proj.dtype),
        scratch_shapes=[pltpu.VMEM((tokens, keys), jnp.float32)],
        cost_estimate=pl.CostEstimate(
            flops=4 * tokens * keys * HD * heads,
            transcendentals=tokens * keys * heads,
            bytes_accessed=2 * (2 * tokens * width + 2 * keys * window.shape[1]),
        ),
    )(base, q_proj, window, window)


def butterfly_sum(value, axis, first, last):
    stride = first
    while stride < last:
        pairs = [(source, source ^ stride) for source in range(lax.axis_size(axis))]
        value = value + lax.ppermute(value, axis, pairs)
        stride *= 2
    return value


def chip_first_sum(value, axis, attend):
    count = lax.axis_size(axis)
    value = butterfly_sum(value, axis, 1, 2)
    half = value.shape[0] // 2
    core = lax.axis_index(axis) % 2
    mine = jnp.where(core == 0, value[:half], value[half:])
    mine = butterfly_sum(mine, axis, 2, 4)
    mine, attended = attend(mine)
    mine = butterfly_sum(mine, axis, 4, count)
    mine, attended = lax.optimization_barrier((mine, attended))
    other = lax.ppermute(mine, axis, [(source, source ^ 1) for source in range(count)])
    both = jnp.where(core == 0, jnp.concatenate([mine, other]), jnp.concatenate([other, mine]))
    return both, attended


def compose(earlier, later, rate3):
    decay = jnp.exp(-rate3 * later[0][None])
    states = decay * earlier[1:] + later[1:]
    return jnp.concatenate([(earlier[0] + later[0])[None], states], axis=0)


def entering_state(step_sum, final_state, rate3):
    inclusive = jnp.concatenate([step_sum[None], final_state], axis=0)
    exclusive = None
    peers = lax.axis_size("seq")
    distance = 1
    while distance < peers:
        received = shifted(inclusive, "seq", distance)
        exclusive = received if exclusive is None else compose(received, exclusive, rate3)
        if distance * 2 < peers:
            inclusive = compose(received, inclusive, rate3)
        distance *= 2
    return exclusive[1:]


def window_blocks(k_proj, v_proj, conv_tail, key_span):
    tokens = k_proj.shape[0]
    own = jnp.concatenate([k_proj, v_proj], axis=1)
    width = own.shape[1]
    tail = conv_tail.reshape(-1, width)
    first = shifted(jnp.concatenate([own, tail], axis=0), "seq", 1)
    tail_in = first[tokens:].reshape(conv_tail.shape)
    held = [first[:tokens], own]
    reach = 2
    while reach * 2 <= key_span:
        held = [shifted(jnp.concatenate(held, axis=0), "seq", reach)] + held
        reach *= 2
    assert reach == key_span
    held = [shifted(own, "seq", key_span)] + held
    return jnp.concatenate(held, axis=0), tail_in


def per_device(
    conv_in,
    gate_in,
    q_proj,
    k_proj,
    v_proj,
    conv_weight,
    conv_bias,
    proj_dt_weight,
    proj_bc_weight,
    dt_gain,
    dt_weight,
    dt_bias,
    decay_rate,
    skip_weight,
):
    tokens_here, channels = conv_in.shape
    key_span = WINDOW // tokens_here
    conv_tail = conv_in[tokens_here - (KCONV - 1) :]
    window, tail_in = window_blocks(k_proj, v_proj, conv_tail, key_span)
    padded = jnp.concatenate([tail_in, conv_in], axis=0).astype(jnp.float32)
    activated = causal_conv(padded, conv_weight, conv_bias, tokens_here)
    state_parts = lax.dot_general(
        proj_bc_weight, activated, (((1,), (1,)), ((), ())), preferred_element_type=jnp.float32
    )
    rank_part = jnp.dot(activated, proj_dt_weight, preferred_element_type=jnp.float32)
    rank_width = rank_part.shape[1]
    packed = jnp.concatenate([rank_part, state_parts.reshape(-1, rank_width)], axis=0)
    base = (lax.axis_index("seq") * tokens_here).astype(jnp.int32).reshape(1)

    def attend(partial):
        partial, ready = lax.optimization_barrier((partial, window))
        return partial, run_attention(q_proj, ready, base)

    total, attn_out = chip_first_sum(packed, "tp", attend)
    rank_low = total[:tokens_here]
    state_in = total[tokens_here:].reshape(state_parts.shape)
    rank_normed = rank_norm(rank_low, dt_gain)
    state_count = decay_rate.shape[0]
    lanes = channels // SUBLANES

    def cube(matrix):
        return matrix.reshape(matrix.shape[:-1] + (SUBLANES, lanes))

    act3 = cube(activated).astype(jnp.float32)
    dt3 = jax.nn.softplus(
        jnp.einsum("tr,rsl->tsl", rank_normed, cube(dt_weight), preferred_element_type=jnp.float32)
        + cube(dt_bias)[None]
    )
    dr3 = dt3 * act3
    rate3 = cube(decay_rate)
    zero_state = jnp.zeros((state_count, SUBLANES, lanes), jnp.float32)
    local_final = run_scan(state_in, dt3, dr3, rate3, zero_state, False)
    step_sum = jnp.sum(dt3, axis=0)
    entering = entering_state(step_sum, local_final, rate3)
    mamba_sum = run_scan(state_in, dt3, dr3, rate3, entering, True)
    mamba_out = (
        ((mamba_sum + cube(skip_weight)[None] * act3) * jax.nn.silu(cube(gate_in).astype(jnp.float32)))
        .astype(jnp.bfloat16)
        .reshape(tokens_here, channels)
    )
    return (mamba_out, attn_out)


def solution(mesh):
    return jax.shard_map(
        per_device,
        mesh=mesh,
        in_specs=(
            P("seq", "tp"),
            P("seq", "tp"),
            P("seq", "tp"),
            P("seq", "tp"),
            P("seq", "tp"),
            P(None, "tp"),
            P("tp"),
            P("tp", None),
            P(None, "tp"),
            P(),
            P(None, "tp"),
            P("tp"),
            P(None, "tp"),
            P("tp"),
        ),
        out_specs=(P("seq", "tp"), P("seq", "tp")),
        check_vma=False,
    )
```

```python
import functools
import math

import jax
import jax.numpy as jnp
from jax import lax
from jax.experimental import pallas as pl
from jax.experimental.pallas import tpu as pltpu
from jax.sharding import PartitionSpec as P

KCONV = 4
HD = 128
WINDOW = 2048
SUBLANES = 8
LANE_BLOCK = 256
epsilon = 1e-06


def shifted(value, axis, steps):
    count = lax.axis_size(axis)
    first, last = (max(0, -steps), min(count, count - steps))
    return lax.ppermute(value, axis, [(source, source + steps) for source in range(first, last)])


def causal_conv(padded, conv_weight, conv_bias, length):
    summed = conv_bias[None, :] + jnp.zeros((length, padded.shape[1]), jnp.float32)
    for offset in range(KCONV):
        summed = summed + conv_weight[offset][None, :] * padded[offset : offset + length]
    return jax.nn.silu(summed).astype(jnp.bfloat16)


def rank_norm(rank_low, dt_gain):
    mean_square = jnp.mean(rank_low * rank_low, axis=-1, keepdims=True)
    return (rank_low * lax.rsqrt(mean_square + epsilon) * dt_gain[None, :]).astype(jnp.bfloat16)


def scan_kernel(with_out, bc_ref, dt_ref, dr_ref, rate_ref, h0_ref, out_ref):
    states = rate_ref.shape[0]
    tokens = dt_ref.shape[0]

    def body(t, hs):
        dt = dt_ref[t]
        dr = dr_ref[t]
        new = []
        acc = None
        for n in range(states):
            h = jnp.exp(rate_ref[n] * dt) * hs[n] + bc_ref[n, t] * dr
            new.append(h)
            if with_out:
                term = bc_ref[states + n, t] * h
                acc = term if acc is None else acc + term
        if with_out:
            out_ref[t] = acc
        return tuple(new)

    hs = lax.fori_loop(0, tokens, body, tuple(h0_ref[n] for n in range(states)), unroll=2)
    if not with_out:
        for n in range(states):
            out_ref[n] = hs[n]


def run_scan(bc, dt3, dr3, rate3, h0, with_out):
    tokens, sub, lanes = dt3.shape
    states = rate3.shape[0]
    blocks = lanes // LANE_BLOCK
    row_spec = pl.BlockSpec((tokens, sub, LANE_BLOCK), lambda j: (0, 0, j))
    state_spec = pl.BlockSpec((states, sub, LANE_BLOCK), lambda j: (0, 0, j))
    out_shape = (tokens, sub, lanes) if with_out else (states, sub, lanes)
    elems = tokens * states * sub * lanes
    return pl.pallas_call(
        functools.partial(scan_kernel, with_out),
        grid=(blocks,),
        in_specs=[
            pl.BlockSpec(memory_space=pltpu.SMEM),
            row_spec,
            row_spec,
            state_spec,
            state_spec,
        ],
        out_specs=row_spec if with_out else state_spec,
        out_shape=jax.ShapeDtypeStruct(out_shape, jnp.float32),
        cost_estimate=pl.CostEstimate(
            flops=(6 if with_out else 4) * elems,
            transcendentals=elems,
            bytes_accessed=4 * (3 * tokens * sub * lanes + 2 * states * sub * lanes),
        ),
    )(bc, dt3, dr3, rate3, h0)


def attention_kernel(base_ref, q_ref, k_ref, v_ref, o_ref, bias_ref):
    @pl.when(pl.program_id(0) == 0)
    def _():
        rows = lax.broadcasted_iota(jnp.int32, bias_ref.shape, 0)
        cols = lax.broadcasted_iota(jnp.int32, bias_ref.shape, 1)
        distance = WINDOW + rows - cols
        in_window = (distance >= 0) & (distance < WINDOW) & (cols + base_ref[0] >= WINDOW)
        bias_ref[...] = jnp.where(in_window, 0.0, -jnp.inf)

    scores = lax.dot_general(
        q_ref[...], k_ref[...], (((1,), (1,)), ((), ())), preferred_element_type=jnp.float32
    ) * (1.0 / math.sqrt(HD)) + bias_ref[...]
    row_peak = jnp.max(scores, axis=1, keepdims=True)
    weights = jnp.exp(scores - row_peak).astype(jnp.bfloat16)
    summed = jnp.sum(weights.astype(jnp.float32), axis=1, keepdims=True)
    weighted = jnp.dot(weights, v_ref[...], preferred_element_type=jnp.float32)
    o_ref[...] = (weighted / summed).astype(o_ref.dtype)


def run_attention(q_proj, window, base):
    tokens, width = q_proj.shape
    keys = window.shape[0]
    heads = width // HD
    group = heads // (window.shape[1] // (2 * HD))
    return pl.pallas_call(
        attention_kernel,
        grid=(heads,),
        in_specs=[
            pl.BlockSpec(memory_space=pltpu.SMEM),
            pl.BlockSpec((tokens, HD), lambda h: (0, h)),
            pl.BlockSpec((keys, HD), lambda h: (0, h // group)),
            pl.BlockSpec((keys, HD), lambda h: (0, window.shape[1] // (2 * HD) + h // group)),
        ],
        out_specs=pl.BlockSpec((tokens, HD), lambda h: (0, h)),
        out_shape=jax.ShapeDtypeStruct((tokens, width), q_proj.dtype),
        scratch_shapes=[pltpu.VMEM((tokens, keys), jnp.float32)],
        cost_estimate=pl.CostEstimate(
            flops=4 * tokens * keys * HD * heads,
            transcendentals=tokens * keys * heads,
            bytes_accessed=2 * (2 * tokens * width + 2 * keys * window.shape[1]),
        ),
    )(base, q_proj, window, window)


def butterfly_sum(value, axis, first, last):
    stride = first
    while stride < last:
        pairs = [(source, source ^ stride) for source in range(lax.axis_size(axis))]
        value = value + lax.ppermute(value, axis, pairs)
        stride *= 2
    return value


def chip_first_sum(value, axis):
    count = lax.axis_size(axis)
    value = butterfly_sum(value, axis, 1, 2)
    half = value.shape[0] // 2
    core = lax.axis_index(axis) % 2
    mine = jnp.where(core == 0, value[:half], value[half:])
    mine = butterfly_sum(mine, axis, 2, count)
    other = lax.ppermute(mine, axis, [(source, source ^ 1) for source in range(count)])
    return jnp.where(core == 0, jnp.concatenate([mine, other]), jnp.concatenate([other, mine]))


def compose(earlier, later, rate3):
    decay = jnp.exp(-rate3 * later[0][None])
    states = decay * earlier[1:] + later[1:]
    return jnp.concatenate([(earlier[0] + later[0])[None], states], axis=0)


def entering_state(step_sum, final_state, rate3):
    inclusive = jnp.concatenate([step_sum[None], final_state], axis=0)
    exclusive = None
    peers = lax.axis_size("seq")
    distance = 1
    while distance < peers:
        received = shifted(inclusive, "seq", distance)
        exclusive = received if exclusive is None else compose(received, exclusive, rate3)
        if distance * 2 < peers:
            inclusive = compose(received, inclusive, rate3)
        distance *= 2
    return exclusive[1:]


def window_blocks(k_proj, v_proj, conv_tail, key_span):
    tokens = k_proj.shape[0]
    own = jnp.concatenate([k_proj, v_proj], axis=1)
    width = own.shape[1]
    tail = conv_tail.reshape(-1, width)
    first = shifted(jnp.concatenate([own, tail], axis=0), "seq", 1)
    tail_in = first[tokens:].reshape(conv_tail.shape)
    held = [first[:tokens], own]
    reach = 2
    while reach * 2 <= key_span:
        held = [shifted(jnp.concatenate(held, axis=0), "seq", reach)] + held
        reach *= 2
    assert reach == key_span
    held = [shifted(own, "seq", key_span)] + held
    return jnp.concatenate(held, axis=0), tail_in


def per_device(
    conv_in,
    gate_in,
    q_proj,
    k_proj,
    v_proj,
    conv_weight,
    conv_bias,
    proj_dt_weight,
    proj_bc_weight,
    dt_gain,
    dt_weight,
    dt_bias,
    decay_rate,
    skip_weight,
):
    tokens_here, channels = conv_in.shape
    key_span = WINDOW // tokens_here
    conv_tail = conv_in[tokens_here - (KCONV - 1) :]
    window, tail_in = window_blocks(k_proj, v_proj, conv_tail, key_span)
    padded = jnp.concatenate([tail_in, conv_in], axis=0).astype(jnp.float32)
    activated = causal_conv(padded, conv_weight, conv_bias, tokens_here)
    state_parts = lax.dot_general(
        proj_bc_weight, activated, (((1,), (1,)), ((), ())), preferred_element_type=jnp.float32
    )
    rank_part = jnp.dot(activated, proj_dt_weight, preferred_element_type=jnp.float32)
    rank_width = rank_part.shape[1]
    packed = jnp.concatenate([rank_part, state_parts.reshape(-1, rank_width)], axis=0)
    total = chip_first_sum(packed, "tp")
    rank_low = total[:tokens_here]
    state_in = total[tokens_here:].reshape(state_parts.shape)
    rank_normed = rank_norm(rank_low, dt_gain)
    state_count = decay_rate.shape[0]
    lanes = channels // SUBLANES

    def cube(matrix):
        return matrix.reshape(matrix.shape[:-1] + (SUBLANES, lanes))

    act3 = cube(activated).astype(jnp.float32)
    dt3 = jax.nn.softplus(
        jnp.einsum("tr,rsl->tsl", rank_normed, cube(dt_weight), preferred_element_type=jnp.float32)
        + cube(dt_bias)[None]
    )
    dr3 = dt3 * act3
    rate3 = cube(decay_rate)
    neg_rate3 = -rate3
    zero_state = jnp.zeros((state_count, SUBLANES, lanes), jnp.float32)
    local_final = run_scan(state_in, dt3, dr3, neg_rate3, zero_state, False)
    step_sum = jnp.sum(dt3, axis=0)
    entering = entering_state(step_sum, local_final, rate3)
    mamba_sum = run_scan(state_in, dt3, dr3, neg_rate3, entering, True)
    mamba_out = (
        ((mamba_sum + cube(skip_weight)[None] * act3) * jax.nn.silu(cube(gate_in).astype(jnp.float32)))
        .astype(jnp.bfloat16)
        .reshape(tokens_here, channels)
    )
    base = (lax.axis_index("seq") * tokens_here).astype(jnp.int32).reshape(1)
    attn_out = run_attention(q_proj, window, base)
    return (mamba_out, attn_out)


def solution(mesh):
    return jax.shard_map(
        per_device,
        mesh=mesh,
        in_specs=(
            P("seq", "tp"),
            P("seq", "tp"),
            P("seq", "tp"),
            P("seq", "tp"),
            P("seq", "tp"),
            P(None, "tp"),
            P("tp"),
            P("tp", None),
            P(None, "tp"),
            P(),
            P(None, "tp"),
            P("tp"),
            P(None, "tp"),
            P("tp"),
        ),
        out_specs=(P("seq", "tp"), P("seq", "tp")),
        check_vma=False,
    )
```

```python
import functools
import math

import jax
import jax.numpy as jnp
from jax import lax
from jax.experimental import pallas as pl
from jax.experimental.pallas import tpu as pltpu
from jax.sharding import PartitionSpec as P

KCONV = 4
HD = 128
WINDOW = 2048
SUBLANES = 8
LANE_BLOCK = 128
epsilon = 1e-06


def shifted(value, axis, steps):
    count = lax.axis_size(axis)
    first, last = (max(0, -steps), min(count, count - steps))
    return lax.ppermute(value, axis, [(source, source + steps) for source in range(first, last)])


def causal_conv(padded, conv_weight, conv_bias, length):
    summed = conv_bias[None, :] + jnp.zeros((length, padded.shape[1]), jnp.float32)
    for offset in range(KCONV):
        summed = summed + conv_weight[offset][None, :] * padded[offset : offset + length]
    return jax.nn.silu(summed).astype(jnp.bfloat16)


def rank_norm(rank_low, dt_gain):
    mean_square = jnp.mean(rank_low * rank_low, axis=-1, keepdims=True)
    return (rank_low * lax.rsqrt(mean_square + epsilon) * dt_gain[None, :]).astype(jnp.bfloat16)


def scan_kernel(with_out, bc_ref, dt_ref, dr_ref, rate_ref, h0_ref, out_ref):
    states = rate_ref.shape[0]
    tokens = dt_ref.shape[0]
    held = [rate_ref[n] for n in range(states)] if with_out else None

    def body(t, hs):
        dt = dt_ref[t]
        dr = dr_ref[t]
        new = []
        acc = None
        for n in range(states):
            rate = held[n] if with_out else rate_ref[n]
            h = jnp.exp(rate * dt) * hs[n] + bc_ref[n, t] * dr
            new.append(h)
            if with_out:
                term = bc_ref[states + n, t] * h
                acc = term if acc is None else acc + term
        if with_out:
            out_ref[t] = acc
        return tuple(new)

    hs = lax.fori_loop(0, tokens, body, tuple(h0_ref[n] for n in range(states)), unroll=2)
    if not with_out:
        for n in range(states):
            out_ref[n] = hs[n]


def run_scan(bc, dt3, dr3, rate3, h0, with_out):
    tokens, sub, lanes = dt3.shape
    states = rate3.shape[0]
    width = LANE_BLOCK if with_out else 2 * LANE_BLOCK
    blocks = lanes // width
    row_spec = pl.BlockSpec((tokens, sub, width), lambda j: (0, 0, j))
    state_spec = pl.BlockSpec((states, sub, width), lambda j: (0, 0, j))
    out_shape = (tokens, sub, lanes) if with_out else (states, sub, lanes)
    elems = tokens * states * sub * lanes
    return pl.pallas_call(
        functools.partial(scan_kernel, with_out),
        grid=(blocks,),
        in_specs=[
            pl.BlockSpec(memory_space=pltpu.SMEM),
            row_spec,
            row_spec,
            state_spec,
            state_spec,
        ],
        out_specs=row_spec if with_out else state_spec,
        out_shape=jax.ShapeDtypeStruct(out_shape, jnp.float32),
        cost_estimate=pl.CostEstimate(
            flops=(6 if with_out else 4) * elems,
            transcendentals=elems,
            bytes_accessed=4 * (3 * tokens * sub * lanes + 2 * states * sub * lanes),
        ),
    )(bc, dt3, dr3, rate3, h0)


def attention_kernel(base_ref, q_ref, k_ref, v_ref, o_ref, bias_ref):
    @pl.when(pl.program_id(0) == 0)
    def _():
        rows = lax.broadcasted_iota(jnp.int32, bias_ref.shape, 0)
        cols = lax.broadcasted_iota(jnp.int32, bias_ref.shape, 1)
        distance = WINDOW + rows - cols
        in_window = (distance >= 0) & (distance < WINDOW) & (cols + base_ref[0] >= WINDOW)
        bias_ref[...] = jnp.where(in_window, 0.0, -jnp.inf)

    scores = lax.dot_general(
        q_ref[...], k_ref[...], (((1,), (1,)), ((), ())), preferred_element_type=jnp.float32
    ) * (1.0 / math.sqrt(HD)) + bias_ref[...]
    row_peak = jnp.max(scores, axis=1, keepdims=True)
    weights = jnp.exp(scores - row_peak).astype(jnp.bfloat16)
    summed = jnp.sum(weights.astype(jnp.float32), axis=1, keepdims=True)
    weighted = jnp.dot(weights, v_ref[...], preferred_element_type=jnp.float32)
    o_ref[...] = (weighted / summed).astype(o_ref.dtype)


def run_attention(q_proj, window, base):
    tokens, width = q_proj.shape
    keys = window.shape[0]
    heads = width // HD
    group = heads // (window.shape[1] // (2 * HD))
    return pl.pallas_call(
        attention_kernel,
        grid=(heads,),
        in_specs=[
            pl.BlockSpec(memory_space=pltpu.SMEM),
            pl.BlockSpec((tokens, HD), lambda h: (0, h)),
            pl.BlockSpec((keys, HD), lambda h: (0, h // group)),
            pl.BlockSpec((keys, HD), lambda h: (0, window.shape[1] // (2 * HD) + h // group)),
        ],
        out_specs=pl.BlockSpec((tokens, HD), lambda h: (0, h)),
        out_shape=jax.ShapeDtypeStruct((tokens, width), q_proj.dtype),
        scratch_shapes=[pltpu.VMEM((tokens, keys), jnp.float32)],
        cost_estimate=pl.CostEstimate(
            flops=4 * tokens * keys * HD * heads,
            transcendentals=tokens * keys * heads,
            bytes_accessed=2 * (2 * tokens * width + 2 * keys * window.shape[1]),
        ),
    )(base, q_proj, window, window)


def butterfly_sum(value, axis, first, last):
    stride = first
    while stride < last:
        pairs = [(source, source ^ stride) for source in range(lax.axis_size(axis))]
        value = value + lax.ppermute(value, axis, pairs)
        stride *= 2
    return value


def chip_first_sum(value, axis):
    count = lax.axis_size(axis)
    value = butterfly_sum(value, axis, 1, 2)
    half = value.shape[0] // 2
    core = lax.axis_index(axis) % 2
    mine = jnp.where(core == 0, value[:half], value[half:])
    mine = butterfly_sum(mine, axis, 2, count)
    other = lax.ppermute(mine, axis, [(source, source ^ 1) for source in range(count)])
    return jnp.where(core == 0, jnp.concatenate([mine, other]), jnp.concatenate([other, mine]))


def compose(earlier, later, rate3):
    decay = jnp.exp(-rate3 * later[0][None])
    states = decay * earlier[1:] + later[1:]
    return jnp.concatenate([(earlier[0] + later[0])[None], states], axis=0)


def entering_state(step_sum, final_state, rate3):
    inclusive = jnp.concatenate([step_sum[None], final_state], axis=0)
    exclusive = None
    peers = lax.axis_size("seq")
    distance = 1
    while distance < peers:
        received = shifted(inclusive, "seq", distance)
        exclusive = received if exclusive is None else compose(received, exclusive, rate3)
        if distance * 2 < peers:
            inclusive = compose(received, inclusive, rate3)
        distance *= 2
    return exclusive[1:]


def window_blocks(k_proj, v_proj, conv_tail, key_span):
    tokens = k_proj.shape[0]
    own = jnp.concatenate([k_proj, v_proj], axis=1)
    width = own.shape[1]
    tail = conv_tail.reshape(-1, width)
    first = shifted(jnp.concatenate([own, tail], axis=0), "seq", 1)
    tail_in = first[tokens:].reshape(conv_tail.shape)
    held = [first[:tokens], own]
    reach = 2
    while reach * 2 <= key_span:
        held = [shifted(jnp.concatenate(held, axis=0), "seq", reach)] + held
        reach *= 2
    assert reach == key_span
    held = [shifted(own, "seq", key_span)] + held
    return jnp.concatenate(held, axis=0), tail_in


def per_device(
    conv_in,
    gate_in,
    q_proj,
    k_proj,
    v_proj,
    conv_weight,
    conv_bias,
    proj_dt_weight,
    proj_bc_weight,
    dt_gain,
    dt_weight,
    dt_bias,
    decay_rate,
    skip_weight,
):
    tokens_here, channels = conv_in.shape
    key_span = WINDOW // tokens_here
    conv_tail = conv_in[tokens_here - (KCONV - 1) :]
    window, tail_in = window_blocks(k_proj, v_proj, conv_tail, key_span)
    padded = jnp.concatenate([tail_in, conv_in], axis=0).astype(jnp.float32)
    activated = causal_conv(padded, conv_weight, conv_bias, tokens_here)
    state_parts = lax.dot_general(
        proj_bc_weight, activated, (((1,), (1,)), ((), ())), preferred_element_type=jnp.float32
    )
    rank_part = jnp.dot(activated, proj_dt_weight, preferred_element_type=jnp.float32)
    rank_width = rank_part.shape[1]
    packed = jnp.concatenate([rank_part, state_parts.reshape(-1, rank_width)], axis=0)
    total = chip_first_sum(packed, "tp")
    rank_low = total[:tokens_here]
    state_in = total[tokens_here:].reshape(state_parts.shape)
    rank_normed = rank_norm(rank_low, dt_gain)
    state_count = decay_rate.shape[0]
    lanes = channels // SUBLANES

    def cube(matrix):
        return matrix.reshape(matrix.shape[:-1] + (SUBLANES, lanes))

    act3 = cube(activated).astype(jnp.float32)
    dt3 = jax.nn.softplus(
        jnp.einsum("tr,rsl->tsl", rank_normed, cube(dt_weight), preferred_element_type=jnp.float32)
        + cube(dt_bias)[None]
    )
    dr3 = dt3 * act3
    rate3 = cube(decay_rate)
    neg_rate3 = -rate3
    zero_state = jnp.zeros((state_count, SUBLANES, lanes), jnp.float32)
    local_final = run_scan(state_in, dt3, dr3, neg_rate3, zero_state, False)
    step_sum = jnp.sum(dt3, axis=0)
    entering = entering_state(step_sum, local_final, rate3)
    mamba_sum = run_scan(state_in, dt3, dr3, neg_rate3, entering, True)
    mamba_out = (
        ((mamba_sum + cube(skip_weight)[None] * act3) * jax.nn.silu(cube(gate_in).astype(jnp.float32)))
        .astype(jnp.bfloat16)
        .reshape(tokens_here, channels)
    )
    base = (lax.axis_index("seq") * tokens_here).astype(jnp.int32).reshape(1)
    attn_out = run_attention(q_proj, window, base)
    return (mamba_out, attn_out)


def solution(mesh):
    return jax.shard_map(
        per_device,
        mesh=mesh,
        in_specs=(
            P("seq", "tp"),
            P("seq", "tp"),
            P("seq", "tp"),
            P("seq", "tp"),
            P("seq", "tp"),
            P(None, "tp"),
            P("tp"),
            P("tp", None),
            P(None, "tp"),
            P(),
            P(None, "tp"),
            P("tp"),
            P(None, "tp"),
            P("tp"),
        ),
        out_specs=(P("seq", "tp"), P("seq", "tp")),
        check_vma=False,
    )
```

```python
import functools
import math

import jax
import jax.numpy as jnp
from jax import lax
from jax.experimental import pallas as pl
from jax.experimental.pallas import tpu as pltpu
from jax.sharding import PartitionSpec as P

KCONV = 4
HD = 128
WINDOW = 2048
SUBLANES = 8
LANE_BLOCK = 128
epsilon = 1e-06


def shifted(value, axis, steps):
    count = lax.axis_size(axis)
    first, last = (max(0, -steps), min(count, count - steps))
    return lax.ppermute(value, axis, [(source, source + steps) for source in range(first, last)])


def causal_conv(padded, conv_weight, conv_bias, length):
    summed = conv_bias[None, :] + jnp.zeros((length, padded.shape[1]), jnp.float32)
    for offset in range(KCONV):
        summed = summed + conv_weight[offset][None, :] * padded[offset : offset + length]
    return jax.nn.silu(summed).astype(jnp.bfloat16)


def rank_norm(rank_low, dt_gain):
    mean_square = jnp.mean(rank_low * rank_low, axis=-1, keepdims=True)
    return (rank_low * lax.rsqrt(mean_square + epsilon) * dt_gain[None, :]).astype(jnp.bfloat16)


def scan_kernel(with_out, bc_ref, dt_ref, dr_ref, rate_ref, h0_ref, *rest):
    if with_out:
        skip_ref, act_ref, gate_ref, out_ref = rest
    else:
        (out_ref,) = rest
    states = rate_ref.shape[0]
    tokens = dt_ref.shape[0]
    held = [rate_ref[n] for n in range(states)] if with_out else None

    def body(t, hs):
        dt = dt_ref[t]
        dr = dr_ref[t]
        new = []
        acc = None
        for n in range(states):
            rate = held[n] if with_out else rate_ref[n]
            h = jnp.exp(rate * dt) * hs[n] + bc_ref[n, t] * dr
            new.append(h)
            if with_out:
                term = bc_ref[states + n, t] * h
                acc = term if acc is None else acc + term
        if with_out:
            out_ref[t] = (acc + skip_ref[...] * act_ref[t]) * gate_ref[t]
        return tuple(new)

    hs = lax.fori_loop(0, tokens, body, tuple(h0_ref[n] for n in range(states)), unroll=2)
    if not with_out:
        for n in range(states):
            out_ref[n] = hs[n]


def run_scan(bc, dt3, dr3, rate3, h0, with_out, extra=()):
    tokens, sub, lanes = dt3.shape
    states = rate3.shape[0]
    width = LANE_BLOCK if with_out else 2 * LANE_BLOCK
    blocks = lanes // width
    row_spec = pl.BlockSpec((tokens, sub, width), lambda j: (0, 0, j))
    state_spec = pl.BlockSpec((states, sub, width), lambda j: (0, 0, j))
    out_shape = (tokens, sub, lanes) if with_out else (states, sub, lanes)
    elems = tokens * states * sub * lanes
    return pl.pallas_call(
        functools.partial(scan_kernel, with_out),
        grid=(blocks,),
        in_specs=[
            pl.BlockSpec(memory_space=pltpu.SMEM),
            row_spec,
            row_spec,
            state_spec,
            state_spec,
        ] + ([pl.BlockSpec((sub, width), lambda j: (0, j)), row_spec, row_spec] if with_out else []),
        out_specs=row_spec if with_out else state_spec,
        out_shape=jax.ShapeDtypeStruct(out_shape, jnp.float32),
        cost_estimate=pl.CostEstimate(
            flops=(6 if with_out else 4) * elems,
            transcendentals=elems,
            bytes_accessed=4 * (3 * tokens * sub * lanes + 2 * states * sub * lanes),
        ),
    )(bc, dt3, dr3, rate3, h0, *extra)


def attention_kernel(base_ref, q_ref, k_ref, v_ref, o_ref, bias_ref):
    @pl.when(pl.program_id(0) == 0)
    def _():
        rows = lax.broadcasted_iota(jnp.int32, bias_ref.shape, 0)
        cols = lax.broadcasted_iota(jnp.int32, bias_ref.shape, 1)
        distance = WINDOW + rows - cols
        in_window = (distance >= 0) & (distance < WINDOW) & (cols + base_ref[0] >= WINDOW)
        bias_ref[...] = jnp.where(in_window, 0.0, -jnp.inf)

    scores = lax.dot_general(
        q_ref[...], k_ref[...], (((1,), (1,)), ((), ())), preferred_element_type=jnp.float32
    ) * (1.0 / math.sqrt(HD)) + bias_ref[...]
    row_peak = jnp.max(scores, axis=1, keepdims=True)
    weights = jnp.exp(scores - row_peak).astype(jnp.bfloat16)
    summed = jnp.sum(weights.astype(jnp.float32), axis=1, keepdims=True)
    weighted = jnp.dot(weights, v_ref[...], preferred_element_type=jnp.float32)
    o_ref[...] = (weighted / summed).astype(o_ref.dtype)


def run_attention(q_proj, window, base):
    tokens, width = q_proj.shape
    keys = window.shape[0]
    heads = width // HD
    group = heads // (window.shape[1] // (2 * HD))
    return pl.pallas_call(
        attention_kernel,
        grid=(heads,),
        in_specs=[
            pl.BlockSpec(memory_space=pltpu.SMEM),
            pl.BlockSpec((tokens, HD), lambda h: (0, h)),
            pl.BlockSpec((keys, HD), lambda h: (0, h // group)),
            pl.BlockSpec((keys, HD), lambda h: (0, window.shape[1] // (2 * HD) + h // group)),
        ],
        out_specs=pl.BlockSpec((tokens, HD), lambda h: (0, h)),
        out_shape=jax.ShapeDtypeStruct((tokens, width), q_proj.dtype),
        scratch_shapes=[pltpu.VMEM((tokens, keys), jnp.float32)],
        cost_estimate=pl.CostEstimate(
            flops=4 * tokens * keys * HD * heads,
            transcendentals=tokens * keys * heads,
            bytes_accessed=2 * (2 * tokens * width + 2 * keys * window.shape[1]),
        ),
    )(base, q_proj, window, window)


def butterfly_sum(value, axis, first, last):
    stride = first
    while stride < last:
        pairs = [(source, source ^ stride) for source in range(lax.axis_size(axis))]
        value = value + lax.ppermute(value, axis, pairs)
        stride *= 2
    return value


def chip_first_sum(value, axis):
    count = lax.axis_size(axis)
    value = butterfly_sum(value, axis, 1, 2)
    half = value.shape[0] // 2
    core = lax.axis_index(axis) % 2
    mine = jnp.where(core == 0, value[:half], value[half:])
    mine = butterfly_sum(mine, axis, 2, count)
    other = lax.ppermute(mine, axis, [(source, source ^ 1) for source in range(count)])
    return jnp.where(core == 0, jnp.concatenate([mine, other]), jnp.concatenate([other, mine]))


def compose(earlier, later, rate3):
    decay = jnp.exp(-rate3 * later[0][None])
    states = decay * earlier[1:] + later[1:]
    return jnp.concatenate([(earlier[0] + later[0])[None], states], axis=0)


def entering_state(step_sum, final_state, rate3):
    inclusive = jnp.concatenate([step_sum[None], final_state], axis=0)
    exclusive = None
    peers = lax.axis_size("seq")
    distance = 1
    while distance < peers:
        received = shifted(inclusive, "seq", distance)
        exclusive = received if exclusive is None else compose(received, exclusive, rate3)
        if distance * 2 < peers:
            inclusive = compose(received, inclusive, rate3)
        distance *= 2
    return exclusive[1:]


def window_blocks(k_proj, v_proj, conv_tail, key_span):
    tokens = k_proj.shape[0]
    own = jnp.concatenate([k_proj, v_proj], axis=1)
    width = own.shape[1]
    tail = conv_tail.reshape(-1, width)
    first = shifted(jnp.concatenate([own, tail], axis=0), "seq", 1)
    tail_in = first[tokens:].reshape(conv_tail.shape)
    held = [first[:tokens], own]
    reach = 2
    while reach * 2 <= key_span:
        held = [shifted(jnp.concatenate(held, axis=0), "seq", reach)] + held
        reach *= 2
    assert reach == key_span
    held = [shifted(own, "seq", key_span)] + held
    return jnp.concatenate(held, axis=0), tail_in


def per_device(
    conv_in,
    gate_in,
    q_proj,
    k_proj,
    v_proj,
    conv_weight,
    conv_bias,
    proj_dt_weight,
    proj_bc_weight,
    dt_gain,
    dt_weight,
    dt_bias,
    decay_rate,
    skip_weight,
):
    tokens_here, channels = conv_in.shape
    key_span = WINDOW // tokens_here
    conv_tail = conv_in[tokens_here - (KCONV - 1) :]
    window, tail_in = window_blocks(k_proj, v_proj, conv_tail, key_span)
    padded = jnp.concatenate([tail_in, conv_in], axis=0).astype(jnp.float32)
    activated = causal_conv(padded, conv_weight, conv_bias, tokens_here)
    state_parts = lax.dot_general(
        proj_bc_weight, activated, (((1,), (1,)), ((), ())), preferred_element_type=jnp.float32
    )
    rank_part = jnp.dot(activated, proj_dt_weight, preferred_element_type=jnp.float32)
    rank_width = rank_part.shape[1]
    packed = jnp.concatenate([rank_part, state_parts.reshape(-1, rank_width)], axis=0)
    total = chip_first_sum(packed, "tp")
    rank_low = total[:tokens_here]
    state_in = total[tokens_here:].reshape(state_parts.shape)
    rank_normed = rank_norm(rank_low, dt_gain)
    state_count = decay_rate.shape[0]
    lanes = channels // SUBLANES

    def cube(matrix):
        return matrix.reshape(matrix.shape[:-1] + (SUBLANES, lanes))

    act3 = cube(activated).astype(jnp.float32)
    dt3 = jax.nn.softplus(
        jnp.einsum("tr,rsl->tsl", rank_normed, cube(dt_weight), preferred_element_type=jnp.float32)
        + cube(dt_bias)[None]
    )
    dr3 = dt3 * act3
    rate3 = cube(decay_rate)
    neg_rate3 = -rate3
    zero_state = jnp.zeros((state_count, SUBLANES, lanes), jnp.float32)
    local_final = run_scan(state_in, dt3, dr3, neg_rate3, zero_state, False)
    step_sum = jnp.sum(dt3, axis=0)
    entering = entering_state(step_sum, local_final, rate3)
    gate3 = jax.nn.silu(cube(gate_in).astype(jnp.float32))
    mixed = run_scan(
        state_in, dt3, dr3, neg_rate3, entering, True, (cube(skip_weight), act3, gate3)
    )
    mamba_out = mixed.astype(jnp.bfloat16).reshape(tokens_here, channels)
    base = (lax.axis_index("seq") * tokens_here).astype(jnp.int32).reshape(1)
    attn_out = run_attention(q_proj, window, base)
    return (mamba_out, attn_out)


def solution(mesh):
    return jax.shard_map(
        per_device,
        mesh=mesh,
        in_specs=(
            P("seq", "tp"),
            P("seq", "tp"),
            P("seq", "tp"),
            P("seq", "tp"),
            P("seq", "tp"),
            P(None, "tp"),
            P("tp"),
            P("tp", None),
            P(None, "tp"),
            P(),
            P(None, "tp"),
            P("tp"),
            P(None, "tp"),
            P("tp"),
        ),
        out_specs=(P("seq", "tp"), P("seq", "tp")),
        check_vma=False,
    )
```

```python
import functools
import math

import jax
import jax.numpy as jnp
from jax import lax
from jax.experimental import pallas as pl
from jax.experimental.pallas import tpu as pltpu
from jax.sharding import PartitionSpec as P

KCONV = 4
HD = 128
WINDOW = 2048
SUBLANES = 8
LANE_BLOCK = 128
epsilon = 1e-06


def shifted(value, axis, steps):
    count = lax.axis_size(axis)
    first, last = (max(0, -steps), min(count, count - steps))
    return lax.ppermute(value, axis, [(source, source + steps) for source in range(first, last)])


def causal_conv(padded, conv_weight, conv_bias, length):
    summed = conv_bias[None, :] + jnp.zeros((length, padded.shape[1]), jnp.float32)
    for offset in range(KCONV):
        summed = summed + conv_weight[offset][None, :] * padded[offset : offset + length]
    return jax.nn.silu(summed).astype(jnp.bfloat16)


def rank_norm(rank_low, dt_gain):
    mean_square = jnp.mean(rank_low * rank_low, axis=-1, keepdims=True)
    return (rank_low * lax.rsqrt(mean_square + epsilon) * dt_gain[None, :]).astype(jnp.bfloat16)


def scan_kernel(with_out, bc_ref, dt_ref, dr_ref, rate_ref, h0_ref, *rest):
    if with_out:
        skip_ref, act_ref, gate_ref, out_ref = rest
    else:
        (out_ref,) = rest
    states = rate_ref.shape[0]
    tokens = dt_ref.shape[0]
    held = [rate_ref[n] for n in range(states)] if with_out else None

    def body(t, hs):
        dt = dt_ref[t]
        dr = dr_ref[t]
        new = []
        acc = None
        for n in range(states):
            rate = held[n] if with_out else rate_ref[n]
            h = jnp.exp(rate * dt) * hs[n] + bc_ref[n, t] * dr
            new.append(h)
            if with_out:
                term = bc_ref[states + n, t] * h
                acc = term if acc is None else acc + term
        if with_out:
            out_ref[t] = (acc + skip_ref[...] * act_ref[t]) * gate_ref[t]
        return tuple(new)

    hs = lax.fori_loop(0, tokens, body, tuple(h0_ref[n] for n in range(states)), unroll=4)
    if not with_out:
        for n in range(states):
            out_ref[n] = hs[n]


def run_scan(bc, dt3, dr3, rate3, h0, with_out, extra=()):
    tokens, sub, lanes = dt3.shape
    states = rate3.shape[0]
    width = LANE_BLOCK if with_out else 2 * LANE_BLOCK
    blocks = lanes // width
    row_spec = pl.BlockSpec((tokens, sub, width), lambda j: (0, 0, j))
    state_spec = pl.BlockSpec((states, sub, width), lambda j: (0, 0, j))
    out_shape = (tokens, sub, lanes) if with_out else (states, sub, lanes)
    elems = tokens * states * sub * lanes
    return pl.pallas_call(
        functools.partial(scan_kernel, with_out),
        grid=(blocks,),
        in_specs=[
            pl.BlockSpec(memory_space=pltpu.SMEM),
            row_spec,
            row_spec,
            state_spec,
            state_spec,
        ] + ([pl.BlockSpec((sub, width), lambda j: (0, j)), row_spec, row_spec] if with_out else []),
        out_specs=row_spec if with_out else state_spec,
        out_shape=jax.ShapeDtypeStruct(out_shape, jnp.float32),
        cost_estimate=pl.CostEstimate(
            flops=(6 if with_out else 4) * elems,
            transcendentals=elems,
            bytes_accessed=4 * (3 * tokens * sub * lanes + 2 * states * sub * lanes),
        ),
    )(bc, dt3, dr3, rate3, h0, *extra)


def attention_kernel(base_ref, q_ref, k_ref, v_ref, o_ref, bias_ref):
    @pl.when(pl.program_id(0) == 0)
    def _():
        rows = lax.broadcasted_iota(jnp.int32, bias_ref.shape, 0)
        cols = lax.broadcasted_iota(jnp.int32, bias_ref.shape, 1)
        distance = WINDOW + rows - cols
        in_window = (distance >= 0) & (distance < WINDOW) & (cols + base_ref[0] >= WINDOW)
        bias_ref[...] = jnp.where(in_window, 0.0, -jnp.inf)

    scores = lax.dot_general(
        q_ref[...], k_ref[...], (((1,), (1,)), ((), ())), preferred_element_type=jnp.float32
    ) * (1.0 / math.sqrt(HD)) + bias_ref[...]
    row_peak = jnp.max(scores, axis=1, keepdims=True)
    weights = jnp.exp(scores - row_peak).astype(jnp.bfloat16)
    summed = jnp.sum(weights.astype(jnp.float32), axis=1, keepdims=True)
    weighted = jnp.dot(weights, v_ref[...], preferred_element_type=jnp.float32)
    o_ref[...] = (weighted / summed).astype(o_ref.dtype)


def run_attention(q_proj, window, base):
    tokens, width = q_proj.shape
    keys = window.shape[0]
    heads = width // HD
    group = heads // (window.shape[1] // (2 * HD))
    return pl.pallas_call(
        attention_kernel,
        grid=(heads,),
        in_specs=[
            pl.BlockSpec(memory_space=pltpu.SMEM),
            pl.BlockSpec((tokens, HD), lambda h: (0, h)),
            pl.BlockSpec((keys, HD), lambda h: (0, h // group)),
            pl.BlockSpec((keys, HD), lambda h: (0, window.shape[1] // (2 * HD) + h // group)),
        ],
        out_specs=pl.BlockSpec((tokens, HD), lambda h: (0, h)),
        out_shape=jax.ShapeDtypeStruct((tokens, width), q_proj.dtype),
        scratch_shapes=[pltpu.VMEM((tokens, keys), jnp.float32)],
        cost_estimate=pl.CostEstimate(
            flops=4 * tokens * keys * HD * heads,
            transcendentals=tokens * keys * heads,
            bytes_accessed=2 * (2 * tokens * width + 2 * keys * window.shape[1]),
        ),
    )(base, q_proj, window, window)


def butterfly_sum(value, axis, first, last):
    stride = first
    while stride < last:
        pairs = [(source, source ^ stride) for source in range(lax.axis_size(axis))]
        value = value + lax.ppermute(value, axis, pairs)
        stride *= 2
    return value


def chip_first_sum(value, axis):
    count = lax.axis_size(axis)
    value = butterfly_sum(value, axis, 1, 2)
    half = value.shape[0] // 2
    core = lax.axis_index(axis) % 2
    mine = jnp.where(core == 0, value[:half], value[half:])
    mine = butterfly_sum(mine, axis, 2, count)
    other = lax.ppermute(mine, axis, [(source, source ^ 1) for source in range(count)])
    return jnp.where(core == 0, jnp.concatenate([mine, other]), jnp.concatenate([other, mine]))


def compose(earlier, later, rate3):
    decay = jnp.exp(-rate3 * later[0][None])
    states = decay * earlier[1:] + later[1:]
    return jnp.concatenate([(earlier[0] + later[0])[None], states], axis=0)


def entering_state(step_sum, final_state, rate3):
    inclusive = jnp.concatenate([step_sum[None], final_state], axis=0)
    exclusive = None
    peers = lax.axis_size("seq")
    distance = 1
    while distance < peers:
        received = shifted(inclusive, "seq", distance)
        exclusive = received if exclusive is None else compose(received, exclusive, rate3)
        if distance * 2 < peers:
            inclusive = compose(received, inclusive, rate3)
        distance *= 2
    return exclusive[1:]


def window_blocks(k_proj, v_proj, conv_tail, key_span):
    tokens = k_proj.shape[0]
    own = jnp.concatenate([k_proj, v_proj], axis=1)
    width = own.shape[1]
    tail = conv_tail.reshape(-1, width)
    first = shifted(jnp.concatenate([own, tail], axis=0), "seq", 1)
    tail_in = first[tokens:].reshape(conv_tail.shape)
    held = [first[:tokens], own]
    reach = 2
    while reach * 2 <= key_span:
        held = [shifted(jnp.concatenate(held, axis=0), "seq", reach)] + held
        reach *= 2
    assert reach == key_span
    held = [shifted(own, "seq", key_span)] + held
    return jnp.concatenate(held, axis=0), tail_in


def per_device(
    conv_in,
    gate_in,
    q_proj,
    k_proj,
    v_proj,
    conv_weight,
    conv_bias,
    proj_dt_weight,
    proj_bc_weight,
    dt_gain,
    dt_weight,
    dt_bias,
    decay_rate,
    skip_weight,
):
    tokens_here, channels = conv_in.shape
    key_span = WINDOW // tokens_here
    conv_tail = conv_in[tokens_here - (KCONV - 1) :]
    window, tail_in = window_blocks(k_proj, v_proj, conv_tail, key_span)
    padded = jnp.concatenate([tail_in, conv_in], axis=0).astype(jnp.float32)
    activated = causal_conv(padded, conv_weight, conv_bias, tokens_here)
    state_parts = lax.dot_general(
        proj_bc_weight, activated, (((1,), (1,)), ((), ())), preferred_element_type=jnp.float32
    )
    rank_part = jnp.dot(activated, proj_dt_weight, preferred_element_type=jnp.float32)
    rank_width = rank_part.shape[1]
    packed = jnp.concatenate([rank_part, state_parts.reshape(-1, rank_width)], axis=0)
    total = chip_first_sum(packed, "tp")
    rank_low = total[:tokens_here]
    state_in = total[tokens_here:].reshape(state_parts.shape)
    rank_normed = rank_norm(rank_low, dt_gain)
    state_count = decay_rate.shape[0]
    lanes = channels // SUBLANES

    def cube(matrix):
        return matrix.reshape(matrix.shape[:-1] + (SUBLANES, lanes))

    act3 = cube(activated).astype(jnp.float32)
    dt3 = jax.nn.softplus(
        jnp.einsum("tr,rsl->tsl", rank_normed, cube(dt_weight), preferred_element_type=jnp.float32)
        + cube(dt_bias)[None]
    )
    dr3 = dt3 * act3
    rate3 = cube(decay_rate)
    neg_rate3 = -rate3
    zero_state = jnp.zeros((state_count, SUBLANES, lanes), jnp.float32)
    local_final = run_scan(state_in, dt3, dr3, neg_rate3, zero_state, False)
    step_sum = jnp.sum(dt3, axis=0)
    entering = entering_state(step_sum, local_final, rate3)
    gate3 = jax.nn.silu(cube(gate_in).astype(jnp.float32))
    mixed = run_scan(
        state_in, dt3, dr3, neg_rate3, entering, True, (cube(skip_weight), act3, gate3)
    )
    mamba_out = mixed.astype(jnp.bfloat16).reshape(tokens_here, channels)
    base = (lax.axis_index("seq") * tokens_here).astype(jnp.int32).reshape(1)
    attn_out = run_attention(q_proj, window, base)
    return (mamba_out, attn_out)


def solution(mesh):
    return jax.shard_map(
        per_device,
        mesh=mesh,
        in_specs=(
            P("seq", "tp"),
            P("seq", "tp"),
            P("seq", "tp"),
            P("seq", "tp"),
            P("seq", "tp"),
            P(None, "tp"),
            P("tp"),
            P("tp", None),
            P(None, "tp"),
            P(),
            P(None, "tp"),
            P("tp"),
            P(None, "tp"),
            P("tp"),
        ),
        out_specs=(P("seq", "tp"), P("seq", "tp")),
        check_vma=False,
    )
```

```python
import functools
import math

import jax
import jax.numpy as jnp
from jax import lax
from jax.experimental import pallas as pl
from jax.experimental.pallas import tpu as pltpu
from jax.sharding import PartitionSpec as P

KCONV = 4
HD = 128
WINDOW = 2048
SUBLANES = 8
LANE_BLOCK = 128
epsilon = 1e-06


def shifted(value, axis, steps):
    count = lax.axis_size(axis)
    first, last = (max(0, -steps), min(count, count - steps))
    return lax.ppermute(value, axis, [(source, source + steps) for source in range(first, last)])


def causal_conv(padded, conv_weight, conv_bias, length):
    summed = conv_bias[None, :] + jnp.zeros((length, padded.shape[1]), jnp.float32)
    for offset in range(KCONV):
        summed = summed + conv_weight[offset][None, :] * padded[offset : offset + length]
    return jax.nn.silu(summed).astype(jnp.bfloat16)


def rank_norm(rank_low, dt_gain):
    mean_square = jnp.mean(rank_low * rank_low, axis=-1, keepdims=True)
    return (rank_low * lax.rsqrt(mean_square + epsilon) * dt_gain[None, :]).astype(jnp.bfloat16)


def scan_kernel(with_out, bc_ref, dt_ref, dr_ref, rate_ref, h0_ref, *rest):
    if with_out:
        skip_ref, act_ref, gate_ref, out_ref = rest
    else:
        (out_ref,) = rest
    states = rate_ref.shape[0]
    tokens = dt_ref.shape[0]
    held = [rate_ref[n] for n in range(states)] if with_out else None

    def body(t, hs):
        dt = dt_ref[t]
        dr = dr_ref[t]
        new = []
        acc = None
        for n in range(states):
            rate = held[n] if with_out else rate_ref[n]
            h = jnp.exp(rate * dt) * hs[n] + bc_ref[n, t] * dr
            new.append(h)
            if with_out:
                term = bc_ref[states + n, t] * h
                acc = term if acc is None else acc + term
        if with_out:
            out_ref[t] = (acc + skip_ref[...] * act_ref[t]) * gate_ref[t]
        return tuple(new)

    hs = lax.fori_loop(0, tokens, body, tuple(h0_ref[n] for n in range(states)), unroll=8)
    if not with_out:
        for n in range(states):
            out_ref[n] = hs[n]


def run_scan(bc, dt3, dr3, rate3, h0, with_out, extra=()):
    tokens, sub, lanes = dt3.shape
    states = rate3.shape[0]
    width = LANE_BLOCK if with_out else 2 * LANE_BLOCK
    blocks = lanes // width
    row_spec = pl.BlockSpec((tokens, sub, width), lambda j: (0, 0, j))
    state_spec = pl.BlockSpec((states, sub, width), lambda j: (0, 0, j))
    out_shape = (tokens, sub, lanes) if with_out else (states, sub, lanes)
    elems = tokens * states * sub * lanes
    return pl.pallas_call(
        functools.partial(scan_kernel, with_out),
        grid=(blocks,),
        in_specs=[
            pl.BlockSpec(memory_space=pltpu.SMEM),
            row_spec,
            row_spec,
            state_spec,
            state_spec,
        ] + ([pl.BlockSpec((sub, width), lambda j: (0, j)), row_spec, row_spec] if with_out else []),
        out_specs=row_spec if with_out else state_spec,
        out_shape=jax.ShapeDtypeStruct(out_shape, jnp.float32),
        cost_estimate=pl.CostEstimate(
            flops=(6 if with_out else 4) * elems,
            transcendentals=elems,
            bytes_accessed=4 * (3 * tokens * sub * lanes + 2 * states * sub * lanes),
        ),
    )(bc, dt3, dr3, rate3, h0, *extra)


def attention_kernel(base_ref, q_ref, k_ref, v_ref, o_ref, bias_ref):
    @pl.when(pl.program_id(0) == 0)
    def _():
        rows = lax.broadcasted_iota(jnp.int32, bias_ref.shape, 0)
        cols = lax.broadcasted_iota(jnp.int32, bias_ref.shape, 1)
        distance = WINDOW + rows - cols
        in_window = (distance >= 0) & (distance < WINDOW) & (cols + base_ref[0] >= WINDOW)
        bias_ref[...] = jnp.where(in_window, 0.0, -jnp.inf)

    scores = lax.dot_general(
        q_ref[...], k_ref[...], (((1,), (1,)), ((), ())), preferred_element_type=jnp.float32
    ) * (1.0 / math.sqrt(HD)) + bias_ref[...]
    row_peak = jnp.max(scores, axis=1, keepdims=True)
    weights = jnp.exp(scores - row_peak).astype(jnp.bfloat16)
    summed = jnp.sum(weights.astype(jnp.float32), axis=1, keepdims=True)
    weighted = jnp.dot(weights, v_ref[...], preferred_element_type=jnp.float32)
    o_ref[...] = (weighted / summed).astype(o_ref.dtype)


def run_attention(q_proj, window, base):
    tokens, width = q_proj.shape
    keys = window.shape[0]
    heads = width // HD
    group = heads // (window.shape[1] // (2 * HD))
    return pl.pallas_call(
        attention_kernel,
        grid=(heads,),
        in_specs=[
            pl.BlockSpec(memory_space=pltpu.SMEM),
            pl.BlockSpec((tokens, HD), lambda h: (0, h)),
            pl.BlockSpec((keys, HD), lambda h: (0, h // group)),
            pl.BlockSpec((keys, HD), lambda h: (0, window.shape[1] // (2 * HD) + h // group)),
        ],
        out_specs=pl.BlockSpec((tokens, HD), lambda h: (0, h)),
        out_shape=jax.ShapeDtypeStruct((tokens, width), q_proj.dtype),
        scratch_shapes=[pltpu.VMEM((tokens, keys), jnp.float32)],
        cost_estimate=pl.CostEstimate(
            flops=4 * tokens * keys * HD * heads,
            transcendentals=tokens * keys * heads,
            bytes_accessed=2 * (2 * tokens * width + 2 * keys * window.shape[1]),
        ),
    )(base, q_proj, window, window)


def butterfly_sum(value, axis, first, last):
    stride = first
    while stride < last:
        pairs = [(source, source ^ stride) for source in range(lax.axis_size(axis))]
        value = value + lax.ppermute(value, axis, pairs)
        stride *= 2
    return value


def chip_first_sum(value, axis):
    count = lax.axis_size(axis)
    value = butterfly_sum(value, axis, 1, 2)
    half = value.shape[0] // 2
    core = lax.axis_index(axis) % 2
    mine = jnp.where(core == 0, value[:half], value[half:])
    mine = butterfly_sum(mine, axis, 2, count)
    other = lax.ppermute(mine, axis, [(source, source ^ 1) for source in range(count)])
    return jnp.where(core == 0, jnp.concatenate([mine, other]), jnp.concatenate([other, mine]))


def compose(earlier, later, rate3):
    decay = jnp.exp(-rate3 * later[0][None])
    states = decay * earlier[1:] + later[1:]
    return jnp.concatenate([(earlier[0] + later[0])[None], states], axis=0)


def entering_state(step_sum, final_state, rate3):
    inclusive = jnp.concatenate([step_sum[None], final_state], axis=0)
    exclusive = None
    peers = lax.axis_size("seq")
    distance = 1
    while distance < peers:
        received = shifted(inclusive, "seq", distance)
        exclusive = received if exclusive is None else compose(received, exclusive, rate3)
        if distance * 2 < peers:
            inclusive = compose(received, inclusive, rate3)
        distance *= 2
    return exclusive[1:]


def window_blocks(k_proj, v_proj, conv_tail, key_span):
    tokens = k_proj.shape[0]
    own = jnp.concatenate([k_proj, v_proj], axis=1)
    width = own.shape[1]
    tail = conv_tail.reshape(-1, width)
    first = shifted(jnp.concatenate([own, tail], axis=0), "seq", 1)
    tail_in = first[tokens:].reshape(conv_tail.shape)
    held = [first[:tokens], own]
    reach = 2
    while reach * 2 <= key_span:
        held = [shifted(jnp.concatenate(held, axis=0), "seq", reach)] + held
        reach *= 2
    assert reach == key_span
    held = [shifted(own, "seq", key_span)] + held
    return jnp.concatenate(held, axis=0), tail_in


def per_device(
    conv_in,
    gate_in,
    q_proj,
    k_proj,
    v_proj,
    conv_weight,
    conv_bias,
    proj_dt_weight,
    proj_bc_weight,
    dt_gain,
    dt_weight,
    dt_bias,
    decay_rate,
    skip_weight,
):
    tokens_here, channels = conv_in.shape
    key_span = WINDOW // tokens_here
    conv_tail = conv_in[tokens_here - (KCONV - 1) :]
    window, tail_in = window_blocks(k_proj, v_proj, conv_tail, key_span)
    padded = jnp.concatenate([tail_in, conv_in], axis=0).astype(jnp.float32)
    activated = causal_conv(padded, conv_weight, conv_bias, tokens_here)
    state_parts = lax.dot_general(
        proj_bc_weight, activated, (((1,), (1,)), ((), ())), preferred_element_type=jnp.float32
    )
    rank_part = jnp.dot(activated, proj_dt_weight, preferred_element_type=jnp.float32)
    rank_width = rank_part.shape[1]
    packed = jnp.concatenate([rank_part, state_parts.reshape(-1, rank_width)], axis=0)
    total = chip_first_sum(packed, "tp")
    rank_low = total[:tokens_here]
    state_in = total[tokens_here:].reshape(state_parts.shape)
    rank_normed = rank_norm(rank_low, dt_gain)
    state_count = decay_rate.shape[0]
    lanes = channels // SUBLANES

    def cube(matrix):
        return matrix.reshape(matrix.shape[:-1] + (SUBLANES, lanes))

    act3 = cube(activated).astype(jnp.float32)
    dt3 = jax.nn.softplus(
        jnp.einsum("tr,rsl->tsl", rank_normed, cube(dt_weight), preferred_element_type=jnp.float32)
        + cube(dt_bias)[None]
    )
    dr3 = dt3 * act3
    rate3 = cube(decay_rate)
    neg_rate3 = -rate3
    zero_state = jnp.zeros((state_count, SUBLANES, lanes), jnp.float32)
    local_final = run_scan(state_in, dt3, dr3, neg_rate3, zero_state, False)
    step_sum = jnp.sum(dt3, axis=0)
    entering = entering_state(step_sum, local_final, rate3)
    gate3 = jax.nn.silu(cube(gate_in).astype(jnp.float32))
    mixed = run_scan(
        state_in, dt3, dr3, neg_rate3, entering, True, (cube(skip_weight), act3, gate3)
    )
    mamba_out = mixed.astype(jnp.bfloat16).reshape(tokens_here, channels)
    base = (lax.axis_index("seq") * tokens_here).astype(jnp.int32).reshape(1)
    attn_out = run_attention(q_proj, window, base)
    return (mamba_out, attn_out)


def solution(mesh):
    return jax.shard_map(
        per_device,
        mesh=mesh,
        in_specs=(
            P("seq", "tp"),
            P("seq", "tp"),
            P("seq", "tp"),
            P("seq", "tp"),
            P("seq", "tp"),
            P(None, "tp"),
            P("tp"),
            P("tp", None),
            P(None, "tp"),
            P(),
            P(None, "tp"),
            P("tp"),
            P(None, "tp"),
            P("tp"),
        ),
        out_specs=(P("seq", "tp"), P("seq", "tp")),
        check_vma=False,
    )
```
